256 devices in a mesh: tok: 32 (over z, x), tp: 8 (over y, core).
Axes of the slice: x: 4, y: 4, z: 8, core: 2. Of those that a mesh axis runs over, the one named last changes fastest.
Arguments:
- tokens: bfloat16 [16384, 8192], P('tok', 'tp'), may hold values from -6 to 6
- frozen_weight: bfloat16 [8192, 2048], P('tp'), may hold values from -0.0625 to 0.0625
- adapter_down_matrices: bfloat16 [256, 8192, 64], P('tok', 'tp'), may hold values from -0.0625 to 0.0625
- adapter_up_matrices: bfloat16 [256, 64, 2048], P('tok', None, 'tp'), may hold values from -0.75 to 0.75
- adapter_per_block: int32 [1024], P('tok'), may hold values from 0 to 255, as said below
- slot_per_adapter: int32 [256], replicated, may hold values from 0 to 255, as said below
- rank_per_adapter: int32 [256], replicated, may hold values from 16 to 64
- output_gradient: bfloat16 [16384, 2048], P('tok', 'tp'), may hold values from -6 to 6
Outputs:
- projected: bfloat16 [16384, 2048], P('tok', 'tp')
- token_gradient: bfloat16 [16384, 8192], P('tok', 'tp')
- grad_down: float32 [256, 8192, 64], P('tok', 'tp')
- grad_up: float32 [256, 64, 2048], P('tok', None, 'tp')
The draws below stay inside these ranges and needn't reach their ends.
Inputs may be any that keep to these rules, and one draw needn't show every extreme that they name: `adapter_per_block`: block b covers tokens b * 16 to (b + 1) * 16 - 1. Among the blocks of one index of tok, at most 2 have adapters stored on any one index of tok (slots k with k // 8 equal), and one index of tok receives exactly 2 such blocks from every index. A permutation: adapter a is stored in slot slot_per_adapter[a] of adapter_down_matrices and adapter_up_matrices.
All inputs are finite; a program needn't handle non-finite values.
Results may differ from the reference program's by a relative error of at most 0.0033.
Values may be sent and summed in bfloat16 or wider, within the bound.
No kernel may reach another device: no remote copies, remote signals or barrier semaphores. Data moves between devices by JAX's collectives and lax.ppermute only.
A program may use at most 128 MiB of HBM per device.

```python
import jax
import jax.numpy as jnp
from jax import lax

MODEL_WIDTH = 8192
KEY_VALUE_WIDTH = 2048
MAX_RANK = 64
ALPHA = 32
BLOCK_TOKENS = 16
ADP_DEV = 8
ADAPTER_TOTAL = 256
TOKENS = 16384
BLOCKS = 1024
CAP = 2


def joint_layout(key):
    owner_count = ADAPTER_TOTAL // ADP_DEV
    per_device = BLOCKS // owner_count
    storage = jax.random.permutation(jax.random.fold_in(key, 101), ADAPTER_TOTAL).astype(jnp.int32)
    popular = jax.random.randint(jax.random.fold_in(key, 102), (), 0, owner_count)
    tickets = jnp.arange(owner_count * CAP, dtype=jnp.int32)
    ticket_owner = tickets // CAP
    device_keys = jax.random.split(jax.random.fold_in(key, 103), owner_count)

    def one_device(device_key):
        first_key, second_key, third_key, fourth_key = jax.random.split(device_key, 4)
        shuffled = jax.random.permutation(first_key, owner_count * CAP).astype(jnp.int32)
        position = jnp.argsort(shuffled).astype(jnp.int32)
        priority = jnp.where(ticket_owner == popular, position - owner_count * CAP, position)
        chosen = jnp.argsort(priority)[:per_device].astype(jnp.int32)
        owner_seq = chosen // CAP
        owner_seq = owner_seq[jax.random.permutation(second_key, per_device)]
        local_pick = jnp.minimum(jax.random.randint(third_key, (per_device,), 0, ADP_DEV), jax.random.randint(fourth_key, (per_device,), 0, ADP_DEV))
        return (owner_seq * ADP_DEV + local_pick).astype(jnp.int32)
    slot_seq = jax.vmap(one_device)(device_keys).reshape(BLOCKS)
    inverse = jnp.argsort(storage).astype(jnp.int32)
    return (storage, inverse[slot_seq].astype(jnp.int32))


def draw_adapter_per_block(key, part):
    return joint_layout(key)[1]


def draw_slot_per_adapter(key, part):
    return joint_layout(key)[0]


def touch_ends(entries, stream_key, low, top_value):
    extent = entries.shape
    place = [jax.random.randint(jax.random.fold_in(stream_key, axis), (), 0, extent[axis]) for axis in range(len(extent))]
    entries = entries.at[tuple(place)].set(low)
    longest = extent.index(max(extent))
    place[longest] = (place[longest] + 1) % extent[longest]
    return entries.at[tuple(place)].set(top_value)


def level_of(rng, dims, pieces, smallest, high):
    loudness = 1.0
    for axis_at, blocks in pieces:
        steps = jax.random.uniform(jax.random.fold_in(jax.random.fold_in(rng, 6), axis_at), (blocks,), jnp.float32, smallest / len(pieces), high / len(pieces))
        loudness = loudness * jnp.repeat(jnp.exp(steps), dims[axis_at] // blocks).reshape((-1,) + (1,) * (len(dims) - 1 - axis_at))
    return loudness


def noise(stream_key, shape, deviation, bound, cuts=(), kind=jnp.bfloat16):
    array = jax.random.normal(stream_key, shape, jnp.float32) * deviation
    if len(cuts) > 0:
        array = level_of(stream_key, shape, cuts, -0.22, 0.18) * array
    return jnp.clip(array, min=-bound, max=bound).astype(kind)


def setup_inputs(seed: int = 0) -> dict:
    keys = jax.random.split(jax.random.key(seed), 9)
    return {
        "tokens": noise(keys[0], (TOKENS, MODEL_WIDTH), 1.0, 6.0, ((0, 32), (1, 8))),
        "frozen_weight": noise(keys[1], (MODEL_WIDTH, KEY_VALUE_WIDTH), MODEL_WIDTH ** -0.5, 0.0625, ((0, 8),)),
        "adapter_down_matrices": noise(keys[2], (ADAPTER_TOTAL, MODEL_WIDTH, MAX_RANK), MODEL_WIDTH ** -0.5, 0.0625, ((0, 32), (1, 8))),
        "adapter_up_matrices": noise(keys[3], (ADAPTER_TOTAL, MAX_RANK, KEY_VALUE_WIDTH), MAX_RANK ** -0.5, 0.75, ((0, 32), (2, 8))),
        "adapter_per_block": draw_adapter_per_block(jax.random.fold_in(keys[8], 71), 0),
        "slot_per_adapter": draw_slot_per_adapter(jax.random.fold_in(keys[8], 71), 0),
        "rank_per_adapter": touch_ends(jax.random.randint(keys[6], (ADAPTER_TOTAL,), MAX_RANK // 4, MAX_RANK + 1), jax.random.fold_in(keys[6], 1), MAX_RANK // 4, MAX_RANK).astype(jnp.int32),
        "output_gradient": noise(keys[7], (TOKENS, KEY_VALUE_WIDTH), 1.0, 6.0, ((0, 32), (1, 8))),
    }


def reference(tokens, frozen_weight, adapter_down_matrices, adapter_up_matrices, adapter_per_block, slot_per_adapter, rank_per_adapter, output_gradient):
    block_count = tokens.shape[0] // BLOCK_TOKENS
    slot_of = slot_per_adapter[adapter_per_block].astype(jnp.int32)
    rank_of = rank_per_adapter[adapter_per_block].astype(jnp.int32)
    scale_of = jnp.float32(ALPHA) / rank_of.astype(jnp.float32)
    keep_cols = jnp.arange(MAX_RANK, dtype=jnp.int32)[None, :] < rank_of[:, None]
    base_out = jnp.dot(tokens, frozen_weight, preferred_element_type=jnp.float32)
    frozen_input_gradient = lax.dot_general(output_gradient, frozen_weight, (((1,), (1,)), ((), ())), preferred_element_type=jnp.float32)
    tok_blocks = tokens.reshape(block_count, BLOCK_TOKENS, MODEL_WIDTH)
    grad_blocks = output_gradient.reshape(block_count, BLOCK_TOKENS, KEY_VALUE_WIDTH)

    def one_block(state_pair, block_item):
        down_matrix_sum, up_matrix_sum = state_pair
        storage_position, adapter_scale, keep, rows_in, grads_in = block_item
        down_matrix = lax.dynamic_index_in_dim(adapter_down_matrices, storage_position, 0, keepdims=False)
        up_matrix = lax.dynamic_index_in_dim(adapter_up_matrices, storage_position, 0, keepdims=False)
        reduced_rows = jnp.where(keep[None, :], jnp.dot(rows_in, down_matrix, preferred_element_type=jnp.float32), 0.0).astype(jnp.bfloat16)
        adapter_increment = adapter_scale * jnp.dot(reduced_rows, up_matrix, preferred_element_type=jnp.float32)
        pulled = lax.dot_general(grads_in, up_matrix, (((1,), (1,)), ((), ())), preferred_element_type=jnp.float32)
        reduced_gradient = (adapter_scale * jnp.where(keep[None, :], pulled, 0.0)).astype(jnp.bfloat16)
        adapter_input_gradient = lax.dot_general(reduced_gradient, down_matrix, (((1,), (1,)), ((), ())), preferred_element_type=jnp.float32)
        down_add = jnp.dot(rows_in.T, reduced_gradient, preferred_element_type=jnp.float32)
        up_add = adapter_scale * jnp.dot(reduced_rows.T, grads_in, preferred_element_type=jnp.float32)
        old_down = lax.dynamic_index_in_dim(down_matrix_sum, storage_position, 0, keepdims=False)
        old_up = lax.dynamic_index_in_dim(up_matrix_sum, storage_position, 0, keepdims=False)
        down_matrix_sum = lax.dynamic_update_index_in_dim(down_matrix_sum, old_down + down_add, storage_position, 0)
        up_matrix_sum = lax.dynamic_update_index_in_dim(up_matrix_sum, old_up + up_add, storage_position, 0)
        return (down_matrix_sum, up_matrix_sum), (adapter_increment, adapter_input_gradient)

    starting_offsets = (jnp.zeros(adapter_down_matrices.shape, jnp.float32), jnp.zeros(adapter_up_matrices.shape, jnp.float32))
    (grad_down, grad_up), (deltas, backs) = lax.scan(one_block, starting_offsets, (slot_of, scale_of, keep_cols, tok_blocks, grad_blocks))
    projected = (base_out + deltas.reshape(tokens.shape[0], KEY_VALUE_WIDTH)).astype(jnp.bfloat16)
    token_gradient = (frozen_input_gradient + backs.reshape(tokens.shape[0], MODEL_WIDTH)).astype(jnp.bfloat16)
    return projected, token_gradient, grad_down, grad_up
```

```python
import jax
import jax.numpy as jnp
from jax import lax
from jax.sharding import PartitionSpec as P

ALPHA = 32
BLOCK_TOKENS = 16


def route(block_slot, number_adapters, capacity):
    owner_ids = block_slot // number_adapters
    block_ids = jnp.arange(block_slot.shape[-1], dtype=jnp.int32)
    earlier = (owner_ids[..., :, None] == owner_ids[..., None, :]) & (
        block_ids[None, :] < block_ids[:, None]
    )
    position = jnp.sum(earlier.astype(jnp.int32), axis=-1)
    return owner_ids * capacity + position


def per_device(
    tokens,
    frozen_weight,
    adapter_down_matrices,
    adapter_up_matrices,
    adapter_per_block,
    slot_per_adapter,
    rank_per_adapter,
    output_gradient,
):
    tok_count = lax.axis_size("tok")
    me = lax.axis_index("tok")
    token_rows, width_portion = tokens.shape
    column_portion = output_gradient.shape[1]
    block_count = adapter_per_block.shape[0]
    number_adapters, _, rank_ceiling = adapter_down_matrices.shape
    capacity = max(2, 2 * block_count // tok_count)
    slots = tok_count * capacity
    row_total = slots * BLOCK_TOKENS
    lane = width_portion + column_portion

    block_slot = jnp.take(slot_per_adapter, adapter_per_block)
    destination = route(block_slot, number_adapters, capacity)
    slot_ids = jnp.arange(slots, dtype=jnp.int32)
    hit = destination[None, :] == slot_ids[:, None]
    filled = jnp.any(hit, axis=1)
    source_block = jnp.sum(jnp.where(hit, jnp.arange(block_count, dtype=jnp.int32)[None, :], 0), axis=1)

    packed = jnp.concatenate(
        [
            tokens.reshape(block_count, BLOCK_TOKENS, width_portion),
            output_gradient.reshape(block_count, BLOCK_TOKENS, column_portion),
        ],
        axis=2,
    )
    send = jnp.where(filled[:, None, None], jnp.take(packed, source_block, axis=0), 0)
    arrived = lax.all_to_all(send, "tok", split_axis=0, concat_axis=0, tiled=True)

    all_blocks = lax.all_gather(adapter_per_block, "tok", axis=0, tiled=False)
    all_slot = jnp.take(slot_per_adapter, all_blocks)
    all_dest = route(all_slot, number_adapters, capacity)
    here = all_dest[:, :, None] == (me * capacity + jnp.arange(capacity, dtype=jnp.int32))[None, None, :]
    slot_local = jnp.where(here, (all_slot % number_adapters)[:, :, None] + 1, 0).sum(axis=1) - 1
    slot_adapter = slot_local.reshape(slots)

    input_rows = arrived[:, :, :width_portion].reshape(row_total, width_portion)
    grad_rows = arrived[:, :, width_portion:].reshape(row_total, column_portion)

    stored_ids = me * number_adapters + jnp.arange(number_adapters, dtype=jnp.int32)
    stored_match = slot_per_adapter[None, :] == stored_ids[:, None]
    stored_rank = jnp.sum(jnp.where(stored_match, rank_per_adapter[None, :], 0), axis=1)
    stored_scale = jnp.where(
        stored_rank > 0, jnp.float32(ALPHA) / jnp.maximum(stored_rank, 1).astype(jnp.float32), 0.0
    )
    chosen = slot_adapter[:, None] == jnp.arange(number_adapters, dtype=jnp.int32)[None, :]
    chosen_rows = jnp.broadcast_to(
        chosen[:, None, :], (slots, BLOCK_TOKENS, number_adapters)
    ).reshape(row_total, number_adapters)
    chosen_float = chosen_rows.astype(jnp.float32)
    row_rank = jnp.sum(jnp.where(chosen_rows, stored_rank[None, :], 0), axis=1)
    scale_per_row = jnp.sum(chosen_float * stored_scale[None, :], axis=1)
    keep_cols = jnp.arange(rank_ceiling, dtype=jnp.int32)[None, :] < row_rank[:, None]

    reduced_every_row = jnp.einsum(
        "ue,meb->umb", input_rows, adapter_down_matrices, preferred_element_type=jnp.float32
    )
    low_part = jnp.sum(reduced_every_row * chosen_float[:, :, None], axis=1)
    gathered_every_row = jnp.einsum(
        "hs,gbs->hgb", grad_rows, adapter_up_matrices, preferred_element_type=jnp.float32
    )
    pull_part = jnp.sum(gathered_every_row * chosen_float[:, :, None], axis=1)
    both = lax.psum(jnp.concatenate([low_part, pull_part], axis=1), "tp")
    low_sum = both[:, :rank_ceiling]
    pull_sum = both[:, rank_ceiling:]
    reduced_rows = jnp.where(keep_cols, low_sum, 0.0).astype(jnp.bfloat16)
    reduced_gradient = (scale_per_row[:, None] * jnp.where(keep_cols, pull_sum, 0.0)).astype(
        jnp.bfloat16
    )
    chosen_half = chosen_rows.astype(jnp.bfloat16)
    reduced_picked = chosen_half[:, :, None] * reduced_rows[:, None, :]
    gradient_picked = chosen_half[:, :, None] * reduced_gradient[:, None, :]
    adapter_increment = scale_per_row[:, None] * jnp.einsum(
        "hnq,nqs->hs", reduced_picked, adapter_up_matrices, preferred_element_type=jnp.float32
    )
    grad_down = jnp.einsum(
        "rd,rak->adk", input_rows, gradient_picked, preferred_element_type=jnp.float32
    )
    grad_up = stored_scale[:, None, None] * jnp.einsum(
        "rak,rc->akc", reduced_picked, grad_rows, preferred_element_type=jnp.float32
    )
    adapter_output_rows = jnp.einsum(
        "ymf,mcf->yc", gradient_picked, adapter_down_matrices, preferred_element_type=jnp.float32
    )
    back = jnp.concatenate(
        [
            adapter_output_rows.reshape(slots, BLOCK_TOKENS, width_portion),
            adapter_increment.reshape(slots, BLOCK_TOKENS, column_portion),
        ],
        axis=2,
    )
    returned = lax.all_to_all(back, "tok", split_axis=0, concat_axis=0, tiled=True)
    mine = jnp.take(returned, destination, axis=0)

    base_out = lax.psum_scatter(
        lax.dot_general(
            frozen_weight, tokens, (((0,), (1,)), ((), ())), preferred_element_type=jnp.float32
        ),
        "tp",
        scatter_dimension=0,
        tiled=True,
    ).T
    frozen_input_gradient = lax.dot_general(
        lax.all_gather(output_gradient, "tp", axis=1, tiled=True),
        frozen_weight,
        (((1,), (1,)), ((), ())),
        preferred_element_type=jnp.float32,
    )
    projected = (
        base_out + mine[:, :, width_portion:].reshape(token_rows, column_portion)
    ).astype(jnp.bfloat16)
    token_gradient = (
        frozen_input_gradient + mine[:, :, :width_portion].reshape(token_rows, width_portion)
    ).astype(jnp.bfloat16)
    return (projected, token_gradient, grad_down, grad_up)


def solution(mesh):
    return jax.shard_map(
        per_device,
        mesh=mesh,
        in_specs=(
            P("tok", "tp"),
            P("tp", None),
            P("tok", "tp", None),
            P("tok", None, "tp"),
            P("tok"),
            P(),
            P(),
            P("tok", "tp"),
        ),
        out_specs=(P("tok", "tp"), P("tok", "tp"), P("tok", "tp", None), P("tok", None, "tp")),
        check_vma=False,
    )
```

```python
import jax
import jax.numpy as jnp
from jax import lax
from jax.sharding import PartitionSpec as P

ALPHA = 32
BLOCK_TOKENS = 16


def route(block_slot, number_adapters, capacity):
    owner_ids = block_slot // number_adapters
    block_ids = jnp.arange(block_slot.shape[-1], dtype=jnp.int32)
    earlier = (owner_ids[..., :, None] == owner_ids[..., None, :]) & (
        block_ids[None, :] < block_ids[:, None]
    )
    position = jnp.sum(earlier.astype(jnp.int32), axis=-1)
    return owner_ids * capacity + position


def per_device(
    tokens,
    frozen_weight,
    adapter_down_matrices,
    adapter_up_matrices,
    adapter_per_block,
    slot_per_adapter,
    rank_per_adapter,
    output_gradient,
):
    tok_count = lax.axis_size("tok")
    me = lax.axis_index("tok")
    token_rows, width_portion = tokens.shape
    column_portion = output_gradient.shape[1]
    block_count = adapter_per_block.shape[0]
    number_adapters, _, rank_ceiling = adapter_down_matrices.shape
    capacity = max(2, 2 * block_count // tok_count)
    slots = tok_count * capacity
    row_total = slots * BLOCK_TOKENS
    lane = width_portion + column_portion

    block_slot = jnp.take(slot_per_adapter, adapter_per_block)
    destination = route(block_slot, number_adapters, capacity)
    local_index = block_slot % number_adapters
    slot_ids = jnp.arange(slots, dtype=jnp.int32)
    hit = destination[None, :] == slot_ids[:, None]
    filled = jnp.any(hit, axis=1)
    source_block = jnp.sum(
        jnp.where(hit, jnp.arange(block_count, dtype=jnp.int32)[None, :], 0), axis=1
    )
    tag = jnp.zeros((block_count, BLOCK_TOKENS, 128), jnp.bfloat16)
    tag = tag.at[:, 0, 0].set((local_index + 1).astype(jnp.bfloat16))
    packed = jnp.concatenate(
        [
            tokens.reshape(block_count, BLOCK_TOKENS, width_portion),
            output_gradient.reshape(block_count, BLOCK_TOKENS, column_portion),
            tag,
        ],
        axis=2,
    )
    send = jnp.where(filled[:, None, None], jnp.take(packed, source_block, axis=0), 0)
    send = send.reshape(tok_count, capacity, BLOCK_TOKENS, lane + 128)

    stored_ids = me * number_adapters + jnp.arange(number_adapters, dtype=jnp.int32)
    stored_match = slot_per_adapter[None, :] == stored_ids[:, None]
    stored_rank = jnp.sum(jnp.where(stored_match, rank_per_adapter[None, :], 0), axis=1)
    stored_scale = jnp.where(
        stored_rank > 0, jnp.float32(ALPHA) / jnp.maximum(stored_rank, 1).astype(jnp.float32), 0.0
    )
    part_rows = tok_count * BLOCK_TOKENS

    def owner_part(arrived, previous):
        slot_adapter = arrived[:, 0, lane].astype(jnp.int32) - 1
        input_rows = arrived[:, :, :width_portion].reshape(part_rows, width_portion)
        grad_rows = arrived[:, :, width_portion:lane].reshape(part_rows, column_portion)
        chosen = slot_adapter[:, None] == jnp.arange(number_adapters, dtype=jnp.int32)[None, :]
        chosen_rows = jnp.broadcast_to(
            chosen[:, None, :], (tok_count, BLOCK_TOKENS, number_adapters)
        ).reshape(part_rows, number_adapters)
        chosen_float = chosen_rows.astype(jnp.float32)
        row_rank = jnp.sum(jnp.where(chosen_rows, stored_rank[None, :], 0), axis=1)
        scale_per_row = jnp.sum(chosen_float * stored_scale[None, :], axis=1)
        keep_cols = jnp.arange(rank_ceiling, dtype=jnp.int32)[None, :] < row_rank[:, None]
        reduced_every_row = jnp.einsum(
            "ue,meb->umb", input_rows, adapter_down_matrices, preferred_element_type=jnp.float32
        )
        low_part = jnp.sum(reduced_every_row * chosen_float[:, :, None], axis=1)
        gathered_every_row = jnp.einsum(
            "hs,gbs->hgb", grad_rows, adapter_up_matrices, preferred_element_type=jnp.float32
        )
        pull_part = jnp.sum(gathered_every_row * chosen_float[:, :, None], axis=1)
        partial_sums = jnp.concatenate([low_part, pull_part], axis=1)
        if previous is not None:
            partial_sums, _ = lax.optimization_barrier((partial_sums, previous))
        both = lax.psum(partial_sums, "tp")
        low_sum = both[:, :rank_ceiling]
        pull_sum = both[:, rank_ceiling:]
        reduced_rows = jnp.where(keep_cols, low_sum, 0.0).astype(jnp.bfloat16)
        reduced_gradient = (
            scale_per_row[:, None] * jnp.where(keep_cols, pull_sum, 0.0)
        ).astype(jnp.bfloat16)
        chosen_half = chosen_rows.astype(jnp.bfloat16)
        reduced_picked = chosen_half[:, :, None] * reduced_rows[:, None, :]
        gradient_picked = chosen_half[:, :, None] * reduced_gradient[:, None, :]
        adapter_increment = scale_per_row[:, None] * jnp.einsum(
            "hnq,nqs->hs", reduced_picked, adapter_up_matrices, preferred_element_type=jnp.float32
        )
        down_add = jnp.einsum(
            "rd,rak->adk", input_rows, gradient_picked, preferred_element_type=jnp.float32
        )
        up_add = jnp.einsum(
            "rak,rc->akc", reduced_picked, grad_rows, preferred_element_type=jnp.float32
        )
        adapter_output_rows = jnp.einsum(
            "ymf,mcf->yc", gradient_picked, adapter_down_matrices, preferred_element_type=jnp.float32
        )
        back = jnp.concatenate(
            [
                adapter_output_rows.reshape(tok_count, BLOCK_TOKENS, width_portion),
                adapter_increment.reshape(tok_count, BLOCK_TOKENS, column_portion),
            ],
            axis=2,
        )
        returned = lax.all_to_all(back, "tok", split_axis=0, concat_axis=0, tiled=True)
        return returned, down_add, up_add, both

    returned_parts = []
    grad_down = None
    grad_up = None
    previous = None
    for position in range(capacity):
        arrived = lax.all_to_all(
            send[:, position], "tok", split_axis=0, concat_axis=0, tiled=True
        )
        returned, down_add, up_add, previous = owner_part(arrived, previous)
        returned_parts.append(returned)
        grad_down = down_add if grad_down is None else grad_down + down_add
        grad_up = up_add if grad_up is None else grad_up + up_add
    grad_up = stored_scale[:, None, None] * grad_up
    returned = jnp.stack(returned_parts, axis=1).reshape(slots, BLOCK_TOKENS, lane)
    mine = jnp.take(returned, destination, axis=0)

    base_out = lax.psum_scatter(
        lax.dot_general(
            frozen_weight, tokens, (((0,), (1,)), ((), ())), preferred_element_type=jnp.float32
        ),
        "tp",
        scatter_dimension=0,
        tiled=True,
    ).T
    frozen_input_gradient = lax.dot_general(
        lax.all_gather(output_gradient, "tp", axis=1, tiled=True),
        frozen_weight,
        (((1,), (1,)), ((), ())),
        preferred_element_type=jnp.float32,
    )
    projected = (
        base_out + mine[:, :, width_portion:].reshape(token_rows, column_portion)
    ).astype(jnp.bfloat16)
    token_gradient = (
        frozen_input_gradient + mine[:, :, :width_portion].reshape(token_rows, width_portion)
    ).astype(jnp.bfloat16)
    return (projected, token_gradient, grad_down, grad_up)


def solution(mesh):
    return jax.shard_map(
        per_device,
        mesh=mesh,
        in_specs=(
            P("tok", "tp"),
            P("tp", None),
            P("tok", "tp", None),
            P("tok", None, "tp"),
            P("tok"),
            P(),
            P(),
            P("tok", "tp"),
        ),
        out_specs=(P("tok", "tp"), P("tok", "tp"), P("tok", "tp", None), P("tok", None, "tp")),
        check_vma=False,
    )
```

```python
import jax
import jax.numpy as jnp
from jax import lax
from jax.sharding import PartitionSpec as P

ALPHA = 32
BLOCK_TOKENS = 16


def route(block_slot, number_adapters, capacity):
    owner_ids = block_slot // number_adapters
    block_ids = jnp.arange(block_slot.shape[-1], dtype=jnp.int32)
    earlier = (owner_ids[..., :, None] == owner_ids[..., None, :]) & (
        block_ids[None, :] < block_ids[:, None]
    )
    position = jnp.sum(earlier.astype(jnp.int32), axis=-1)
    return owner_ids * capacity + position


def tree_sum(value, axis):
    size = lax.axis_size(axis)
    step = 1
    while step < size:
        pairs = [(i, i ^ step) for i in range(size)]
        value = value + lax.ppermute(value, axis, pairs)
        step *= 2
    return value


def per_device(
    tokens,
    frozen_weight,
    adapter_down_matrices,
    adapter_up_matrices,
    adapter_per_block,
    slot_per_adapter,
    rank_per_adapter,
    output_gradient,
):
    tok_count = lax.axis_size("tok")
    me = lax.axis_index("tok")
    token_rows, width_portion = tokens.shape
    column_portion = output_gradient.shape[1]
    block_count = adapter_per_block.shape[0]
    number_adapters, _, rank_ceiling = adapter_down_matrices.shape
    capacity = max(2, 2 * block_count // tok_count)
    slots = tok_count * capacity
    row_total = slots * BLOCK_TOKENS
    lane = width_portion + column_portion

    block_slot = jnp.take(slot_per_adapter, adapter_per_block)
    destination = route(block_slot, number_adapters, capacity)
    local_index = block_slot % number_adapters
    slot_ids = jnp.arange(slots, dtype=jnp.int32)
    hit = destination[None, :] == slot_ids[:, None]
    filled = jnp.any(hit, axis=1)
    source_block = jnp.sum(
        jnp.where(hit, jnp.arange(block_count, dtype=jnp.int32)[None, :], 0), axis=1
    )
    tag = jnp.zeros((block_count, BLOCK_TOKENS, 128), jnp.bfloat16)
    tag = tag.at[:, 0, 0].set((local_index + 1).astype(jnp.bfloat16))
    packed = jnp.concatenate(
        [
            tokens.reshape(block_count, BLOCK_TOKENS, width_portion),
            output_gradient.reshape(block_count, BLOCK_TOKENS, column_portion),
            tag,
        ],
        axis=2,
    )
    send = jnp.where(filled[:, None, None], jnp.take(packed, source_block, axis=0), 0)
    send = send.reshape(tok_count, capacity, BLOCK_TOKENS, lane + 128)

    stored_ids = me * number_adapters + jnp.arange(number_adapters, dtype=jnp.int32)
    stored_match = slot_per_adapter[None, :] == stored_ids[:, None]
    stored_rank = jnp.sum(jnp.where(stored_match, rank_per_adapter[None, :], 0), axis=1)
    stored_scale = jnp.where(
        stored_rank > 0, jnp.float32(ALPHA) / jnp.maximum(stored_rank, 1).astype(jnp.float32), 0.0
    )
    part_rows = tok_count * BLOCK_TOKENS

    def owner_part(arrived, previous):
        slot_adapter = arrived[:, 0, lane].astype(jnp.int32) - 1
        input_rows = arrived[:, :, :width_portion].reshape(part_rows, width_portion)
        grad_rows = arrived[:, :, width_portion:lane].reshape(part_rows, column_portion)
        chosen = slot_adapter[:, None] == jnp.arange(number_adapters, dtype=jnp.int32)[None, :]
        chosen_rows = jnp.broadcast_to(
            chosen[:, None, :], (tok_count, BLOCK_TOKENS, number_adapters)
        ).reshape(part_rows, number_adapters)
        chosen_float = chosen_rows.astype(jnp.float32)
        row_rank = jnp.sum(jnp.where(chosen_rows, stored_rank[None, :], 0), axis=1)
        scale_per_row = jnp.sum(chosen_float * stored_scale[None, :], axis=1)
        keep_cols = jnp.arange(rank_ceiling, dtype=jnp.int32)[None, :] < row_rank[:, None]
        reduced_every_row = jnp.einsum(
            "ue,meb->umb", input_rows, adapter_down_matrices, preferred_element_type=jnp.float32
        )
        low_part = jnp.sum(reduced_every_row * chosen_float[:, :, None], axis=1)
        gathered_every_row = jnp.einsum(
            "hs,gbs->hgb", grad_rows, adapter_up_matrices, preferred_element_type=jnp.float32
        )
        pull_part = jnp.sum(gathered_every_row * chosen_float[:, :, None], axis=1)
        partial_sums = jnp.concatenate([low_part, pull_part], axis=1)
        if previous is not None:
            partial_sums, _ = lax.optimization_barrier((partial_sums, previous))
        both = tree_sum(partial_sums, "tp")
        low_sum = both[:, :rank_ceiling]
        pull_sum = both[:, rank_ceiling:]
        reduced_rows = jnp.where(keep_cols, low_sum, 0.0).astype(jnp.bfloat16)
        reduced_gradient = (
            scale_per_row[:, None] * jnp.where(keep_cols, pull_sum, 0.0)
        ).astype(jnp.bfloat16)
        chosen_half = chosen_rows.astype(jnp.bfloat16)
        reduced_picked = chosen_half[:, :, None] * reduced_rows[:, None, :]
        gradient_picked = chosen_half[:, :, None] * reduced_gradient[:, None, :]
        adapter_increment = scale_per_row[:, None] * jnp.einsum(
            "hnq,nqs->hs", reduced_picked, adapter_up_matrices, preferred_element_type=jnp.float32
        )
        down_add = jnp.einsum(
            "rd,rak->adk", input_rows, gradient_picked, preferred_element_type=jnp.float32
        )
        up_add = jnp.einsum(
            "rak,rc->akc", reduced_picked, grad_rows, preferred_element_type=jnp.float32
        )
        adapter_output_rows = jnp.einsum(
            "ymf,mcf->yc", gradient_picked, adapter_down_matrices, preferred_element_type=jnp.float32
        )
        back = jnp.concatenate(
            [
                adapter_output_rows.reshape(tok_count, BLOCK_TOKENS, width_portion),
                adapter_increment.reshape(tok_count, BLOCK_TOKENS, column_portion),
            ],
            axis=2,
        )
        returned = lax.all_to_all(back, "tok", split_axis=0, concat_axis=0, tiled=True)
        return returned, down_add, up_add, both

    returned_parts = []
    grad_down = None
    grad_up = None
    previous = None
    for position in range(capacity):
        arrived = lax.all_to_all(
            send[:, position], "tok", split_axis=0, concat_axis=0, tiled=True
        )
        returned, down_add, up_add, previous = owner_part(arrived, previous)
        returned_parts.append(returned)
        grad_down = down_add if grad_down is None else grad_down + down_add
        grad_up = up_add if grad_up is None else grad_up + up_add
    grad_up = stored_scale[:, None, None] * grad_up
    returned = jnp.stack(returned_parts, axis=1).reshape(slots, BLOCK_TOKENS, lane)
    mine = jnp.take(returned, destination, axis=0)

    base_out = lax.psum_scatter(
        lax.dot_general(
            frozen_weight, tokens, (((0,), (1,)), ((), ())), preferred_element_type=jnp.float32
        ),
        "tp",
        scatter_dimension=0,
        tiled=True,
    ).T
    frozen_input_gradient = lax.dot_general(
        lax.all_gather(output_gradient, "tp", axis=1, tiled=True),
        frozen_weight,
        (((1,), (1,)), ((), ())),
        preferred_element_type=jnp.float32,
    )
    projected = (
        base_out + mine[:, :, width_portion:].reshape(token_rows, column_portion)
    ).astype(jnp.bfloat16)
    token_gradient = (
        frozen_input_gradient + mine[:, :, :width_portion].reshape(token_rows, width_portion)
    ).astype(jnp.bfloat16)
    return (projected, token_gradient, grad_down, grad_up)


def solution(mesh):
    return jax.shard_map(
        per_device,
        mesh=mesh,
        in_specs=(
            P("tok", "tp"),
            P("tp", None),
            P("tok", "tp", None),
            P("tok", None, "tp"),
            P("tok"),
            P(),
            P(),
            P("tok", "tp"),
        ),
        out_specs=(P("tok", "tp"), P("tok", "tp"), P("tok", "tp", None), P("tok", None, "tp")),
        check_vma=False,
    )
```

```python
import jax
import jax.numpy as jnp
from jax import lax
from jax.sharding import PartitionSpec as P

ALPHA = 32
BLOCK_TOKENS = 16


def route(block_slot, number_adapters, capacity):
    owner_ids = block_slot // number_adapters
    block_ids = jnp.arange(block_slot.shape[-1], dtype=jnp.int32)
    earlier = (owner_ids[..., :, None] == owner_ids[..., None, :]) & (
        block_ids[None, :] < block_ids[:, None]
    )
    position = jnp.sum(earlier.astype(jnp.int32), axis=-1)
    return owner_ids * capacity + position


def tree_sum(value, axis):
    size = lax.axis_size(axis)
    step = 1
    while step < size:
        pairs = [(i, i ^ step) for i in range(size)]
        value = value + lax.ppermute(value, axis, pairs)
        step *= 2
    return value


def tree_gather(value, axis):
    size = lax.axis_size(axis)
    me = lax.axis_index(axis)
    value = value[None]
    step = 1
    while step < size:
        pairs = [(i, i ^ step) for i in range(size)]
        other = lax.ppermute(value, axis, pairs)
        low_side = (me & step) == 0
        value = jnp.where(
            low_side,
            jnp.concatenate([value, other], axis=0),
            jnp.concatenate([other, value], axis=0),
        )
        step *= 2
    return value


def per_device(
    tokens,
    frozen_weight,
    adapter_down_matrices,
    adapter_up_matrices,
    adapter_per_block,
    slot_per_adapter,
    rank_per_adapter,
    output_gradient,
):
    tok_count = lax.axis_size("tok")
    tp_count = lax.axis_size("tp")
    me = lax.axis_index("tok")
    token_rows, width_portion = tokens.shape
    column_portion = output_gradient.shape[1]
    block_count = adapter_per_block.shape[0]
    number_adapters, _, rank_ceiling = adapter_down_matrices.shape
    capacity = max(2, 2 * block_count // tok_count)
    slots = tok_count * capacity
    row_total = slots * BLOCK_TOKENS
    lane = width_portion + column_portion

    block_slot = jnp.take(slot_per_adapter, adapter_per_block)
    destination = route(block_slot, number_adapters, capacity)
    local_index = block_slot % number_adapters
    slot_ids = jnp.arange(slots, dtype=jnp.int32)
    hit = destination[None, :] == slot_ids[:, None]
    filled = jnp.any(hit, axis=1)
    source_block = jnp.sum(
        jnp.where(hit, jnp.arange(block_count, dtype=jnp.int32)[None, :], 0), axis=1
    )
    tag = jnp.zeros((block_count, BLOCK_TOKENS, 128), jnp.bfloat16)
    tag = tag.at[:, 0, 0].set((local_index + 1).astype(jnp.bfloat16))
    packed = jnp.concatenate(
        [
            tokens.reshape(block_count, BLOCK_TOKENS, width_portion),
            output_gradient.reshape(block_count, BLOCK_TOKENS, column_portion),
            tag,
        ],
        axis=2,
    )
    send = jnp.where(filled[:, None, None], jnp.take(packed, source_block, axis=0), 0)
    send = send.reshape(tok_count, capacity, BLOCK_TOKENS, lane + 128)

    stored_ids = me * number_adapters + jnp.arange(number_adapters, dtype=jnp.int32)
    stored_match = slot_per_adapter[None, :] == stored_ids[:, None]
    stored_rank = jnp.sum(jnp.where(stored_match, rank_per_adapter[None, :], 0), axis=1)
    stored_scale = jnp.where(
        stored_rank > 0, jnp.float32(ALPHA) / jnp.maximum(stored_rank, 1).astype(jnp.float32), 0.0
    )
    part_rows = tok_count * BLOCK_TOKENS

    def owner_part(arrived, previous):
        slot_adapter = arrived[:, 0, lane].astype(jnp.int32) - 1
        input_rows = arrived[:, :, :width_portion].reshape(part_rows, width_portion)
        grad_rows = arrived[:, :, width_portion:lane].reshape(part_rows, column_portion)
        chosen = slot_adapter[:, None] == jnp.arange(number_adapters, dtype=jnp.int32)[None, :]
        chosen_rows = jnp.broadcast_to(
            chosen[:, None, :], (tok_count, BLOCK_TOKENS, number_adapters)
        ).reshape(part_rows, number_adapters)
        chosen_float = chosen_rows.astype(jnp.float32)
        row_rank = jnp.sum(jnp.where(chosen_rows, stored_rank[None, :], 0), axis=1)
        scale_per_row = jnp.sum(chosen_float * stored_scale[None, :], axis=1)
        keep_cols = jnp.arange(rank_ceiling, dtype=jnp.int32)[None, :] < row_rank[:, None]
        reduced_every_row = jnp.einsum(
            "ue,meb->umb", input_rows, adapter_down_matrices, preferred_element_type=jnp.float32
        )
        low_part = jnp.sum(reduced_every_row * chosen_float[:, :, None], axis=1)
        gathered_every_row = jnp.einsum(
            "hs,gbs->hgb", grad_rows, adapter_up_matrices, preferred_element_type=jnp.float32
        )
        pull_part = jnp.sum(gathered_every_row * chosen_float[:, :, None], axis=1)
        partial_sums = jnp.concatenate([low_part, pull_part], axis=1)
        if previous is not None:
            partial_sums, _ = lax.optimization_barrier((partial_sums, previous))
        both = tree_sum(partial_sums, "tp")
        low_sum = both[:, :rank_ceiling]
        pull_sum = both[:, rank_ceiling:]
        reduced_rows = jnp.where(keep_cols, low_sum, 0.0).astype(jnp.bfloat16)
        reduced_gradient = (
            scale_per_row[:, None] * jnp.where(keep_cols, pull_sum, 0.0)
        ).astype(jnp.bfloat16)
        chosen_half = chosen_rows.astype(jnp.bfloat16)
        reduced_picked = chosen_half[:, :, None] * reduced_rows[:, None, :]
        gradient_picked = chosen_half[:, :, None] * reduced_gradient[:, None, :]
        adapter_increment = scale_per_row[:, None] * jnp.einsum(
            "hnq,nqs->hs", reduced_picked, adapter_up_matrices, preferred_element_type=jnp.float32
        )
        down_add = jnp.einsum(
            "rd,rak->adk", input_rows, gradient_picked, preferred_element_type=jnp.float32
        )
        up_add = jnp.einsum(
            "rak,rc->akc", reduced_picked, grad_rows, preferred_element_type=jnp.float32
        )
        adapter_output_rows = jnp.einsum(
            "ymf,mcf->yc", gradient_picked, adapter_down_matrices, preferred_element_type=jnp.float32
        )
        every_column = tree_gather(grad_rows, "tp")
        frozen_part = lax.dot_general(
            jnp.moveaxis(every_column, 0, 1).reshape(part_rows, tp_count * column_portion),
            frozen_weight,
            (((1,), (1,)), ((), ())),
            preferred_element_type=jnp.float32,
        )
        gradient_rows = (frozen_part + adapter_output_rows).astype(jnp.bfloat16)
        increment_high = adapter_increment.astype(jnp.bfloat16)
        increment_low = (adapter_increment - increment_high.astype(jnp.float32)).astype(
            jnp.bfloat16
        )
        back = jnp.concatenate(
            [
                gradient_rows.reshape(tok_count, BLOCK_TOKENS, width_portion),
                increment_high.reshape(tok_count, BLOCK_TOKENS, column_portion),
                increment_low.reshape(tok_count, BLOCK_TOKENS, column_portion),
            ],
            axis=2,
        )
        returned = lax.all_to_all(back, "tok", split_axis=0, concat_axis=0, tiled=True)
        return returned, down_add, up_add, both

    returned_parts = []
    grad_down = None
    grad_up = None
    previous = None
    for position in range(capacity):
        arrived = lax.all_to_all(
            send[:, position], "tok", split_axis=0, concat_axis=0, tiled=True
        )
        returned, down_add, up_add, previous = owner_part(arrived, previous)
        returned_parts.append(returned)
        grad_down = down_add if grad_down is None else grad_down + down_add
        grad_up = up_add if grad_up is None else grad_up + up_add
    grad_up = stored_scale[:, None, None] * grad_up
    returned = jnp.stack(returned_parts, axis=1).reshape(
        slots, BLOCK_TOKENS, width_portion + 2 * column_portion
    )
    mine = jnp.take(returned, destination, axis=0)

    base_out = lax.psum_scatter(
        lax.dot_general(
            frozen_weight, tokens, (((0,), (1,)), ((), ())), preferred_element_type=jnp.float32
        ),
        "tp",
        scatter_dimension=0,
        tiled=True,
    ).T
    increment = mine[:, :, width_portion : width_portion + column_portion].astype(
        jnp.float32
    ) + mine[:, :, width_portion + column_portion :].astype(jnp.float32)
    projected = (base_out + increment.reshape(token_rows, column_portion)).astype(jnp.bfloat16)
    token_gradient = mine[:, :, :width_portion].reshape(token_rows, width_portion)
    return (projected, token_gradient, grad_down, grad_up)


def solution(mesh):
    return jax.shard_map(
        per_device,
        mesh=mesh,
        in_specs=(
            P("tok", "tp"),
            P("tp", None),
            P("tok", "tp", None),
            P("tok", None, "tp"),
            P("tok"),
            P(),
            P(),
            P("tok", "tp"),
        ),
        out_specs=(P("tok", "tp"), P("tok", "tp"), P("tok", "tp", None), P("tok", None, "tp")),
        check_vma=False,
    )
```

```python
import jax
import jax.numpy as jnp
from jax import lax
from jax.sharding import PartitionSpec as P

ALPHA = 32
BLOCK_TOKENS = 16


def route(block_slot, number_adapters, capacity):
    owner_ids = block_slot // number_adapters
    block_ids = jnp.arange(block_slot.shape[-1], dtype=jnp.int32)
    earlier = (owner_ids[..., :, None] == owner_ids[..., None, :]) & (
        block_ids[None, :] < block_ids[:, None]
    )
    position = jnp.sum(earlier.astype(jnp.int32), axis=-1)
    return owner_ids * capacity + position


def tree_sum(value, axis):
    size = lax.axis_size(axis)
    step = 1
    while step < size:
        pairs = [(i, i ^ step) for i in range(size)]
        value = value + lax.ppermute(value, axis, pairs)
        step *= 2
    return value


def tree_gather(value, axis):
    size = lax.axis_size(axis)
    me = lax.axis_index(axis)
    value = value[None]
    step = 1
    while step < size:
        pairs = [(i, i ^ step) for i in range(size)]
        other = lax.ppermute(value, axis, pairs)
        low_side = (me & step) == 0
        value = jnp.where(
            low_side,
            jnp.concatenate([value, other], axis=0),
            jnp.concatenate([other, value], axis=0),
        )
        step *= 2
    return value


def per_device(
    tokens,
    frozen_weight,
    adapter_down_matrices,
    adapter_up_matrices,
    adapter_per_block,
    slot_per_adapter,
    rank_per_adapter,
    output_gradient,
):
    tok_count = lax.axis_size("tok")
    tp_count = lax.axis_size("tp")
    me = lax.axis_index("tok")
    token_rows, width_portion = tokens.shape
    column_portion = output_gradient.shape[1]
    block_count = adapter_per_block.shape[0]
    number_adapters, _, rank_ceiling = adapter_down_matrices.shape
    capacity = max(2, 2 * block_count // tok_count)
    slots = tok_count * capacity
    row_total = slots * BLOCK_TOKENS
    lane = width_portion + column_portion

    block_slot = jnp.take(slot_per_adapter, adapter_per_block)
    destination = route(block_slot, number_adapters, capacity)
    local_index = block_slot % number_adapters
    slot_ids = jnp.arange(slots, dtype=jnp.int32)
    hit = destination[None, :] == slot_ids[:, None]
    filled = jnp.any(hit, axis=1)
    source_block = jnp.sum(
        jnp.where(hit, jnp.arange(block_count, dtype=jnp.int32)[None, :], 0), axis=1
    )
    tag = jnp.zeros((block_count, BLOCK_TOKENS, 128), jnp.bfloat16)
    tag = tag.at[:, 0, 0].set((local_index + 1).astype(jnp.bfloat16))
    packed = jnp.concatenate(
        [
            tokens.reshape(block_count, BLOCK_TOKENS, width_portion),
            output_gradient.reshape(block_count, BLOCK_TOKENS, column_portion),
            tag,
        ],
        axis=2,
    )
    send = jnp.where(filled[:, None, None], jnp.take(packed, source_block, axis=0), 0)
    send = send.reshape(tok_count, capacity, BLOCK_TOKENS, lane + 128)

    stored_ids = me * number_adapters + jnp.arange(number_adapters, dtype=jnp.int32)
    stored_match = slot_per_adapter[None, :] == stored_ids[:, None]
    stored_rank = jnp.sum(jnp.where(stored_match, rank_per_adapter[None, :], 0), axis=1)
    stored_scale = jnp.where(
        stored_rank > 0, jnp.float32(ALPHA) / jnp.maximum(stored_rank, 1).astype(jnp.float32), 0.0
    )
    part_rows = tok_count * BLOCK_TOKENS

    def owner_part(arrived, previous):
        slot_adapter = arrived[:, 0, lane].astype(jnp.int32) - 1
        input_rows = arrived[:, :, :width_portion].reshape(part_rows, width_portion)
        grad_rows = arrived[:, :, width_portion:lane].reshape(part_rows, column_portion)
        chosen = slot_adapter[:, None] == jnp.arange(number_adapters, dtype=jnp.int32)[None, :]
        chosen_rows = jnp.broadcast_to(
            chosen[:, None, :], (tok_count, BLOCK_TOKENS, number_adapters)
        ).reshape(part_rows, number_adapters)
        chosen_float = chosen_rows.astype(jnp.float32)
        row_rank = jnp.sum(jnp.where(chosen_rows, stored_rank[None, :], 0), axis=1)
        scale_per_row = jnp.sum(chosen_float * stored_scale[None, :], axis=1)
        keep_cols = jnp.arange(rank_ceiling, dtype=jnp.int32)[None, :] < row_rank[:, None]
        reduced_every_row = jnp.einsum(
            "ue,meb->umb", input_rows, adapter_down_matrices, preferred_element_type=jnp.float32
        )
        low_part = jnp.sum(reduced_every_row * chosen_float[:, :, None], axis=1)
        gathered_every_row = jnp.einsum(
            "hs,gbs->hgb", grad_rows, adapter_up_matrices, preferred_element_type=jnp.float32
        )
        pull_part = jnp.sum(gathered_every_row * chosen_float[:, :, None], axis=1)
        partial_sums = jnp.concatenate([low_part, pull_part], axis=1)
        if previous is not None:
            partial_sums, _ = lax.optimization_barrier((partial_sums, previous))
        both = tree_sum(partial_sums, "tp")
        low_sum = both[:, :rank_ceiling]
        pull_sum = both[:, rank_ceiling:]
        reduced_rows = jnp.where(keep_cols, low_sum, 0.0).astype(jnp.bfloat16)
        reduced_gradient = (
            scale_per_row[:, None] * jnp.where(keep_cols, pull_sum, 0.0)
        ).astype(jnp.bfloat16)
        chosen_half = chosen_rows.astype(jnp.bfloat16)
        reduced_picked = chosen_half[:, :, None] * reduced_rows[:, None, :]
        gradient_picked = chosen_half[:, :, None] * reduced_gradient[:, None, :]
        adapter_increment = scale_per_row[:, None] * jnp.einsum(
            "hnq,nqs->hs", reduced_picked, adapter_up_matrices, preferred_element_type=jnp.float32
        )
        down_add = jnp.einsum(
            "rd,rak->adk", input_rows, gradient_picked, preferred_element_type=jnp.float32
        )
        up_add = jnp.einsum(
            "rak,rc->akc", reduced_picked, grad_rows, preferred_element_type=jnp.float32
        )
        adapter_output_rows = jnp.einsum(
            "ymf,mcf->yc", gradient_picked, adapter_down_matrices, preferred_element_type=jnp.float32
        )
        every_column = tree_gather(grad_rows, "tp")
        frozen_part = lax.dot_general(
            jnp.moveaxis(every_column, 0, 1).reshape(part_rows, tp_count * column_portion),
            frozen_weight,
            (((1,), (1,)), ((), ())),
            preferred_element_type=jnp.float32,
        )
        gradient_rows = (frozen_part + adapter_output_rows).astype(jnp.bfloat16)
        increment_round = lax.reduce_precision(adapter_increment, exponent_bits=8, mantissa_bits=7)
        increment_high = increment_round.astype(jnp.bfloat16)
        increment_low = (adapter_increment - increment_round).astype(jnp.bfloat16)
        back = jnp.concatenate(
            [
                gradient_rows.reshape(tok_count, BLOCK_TOKENS, width_portion),
                increment_high.reshape(tok_count, BLOCK_TOKENS, column_portion),
                increment_low.reshape(tok_count, BLOCK_TOKENS, column_portion),
            ],
            axis=2,
        )
        returned = lax.all_to_all(back, "tok", split_axis=0, concat_axis=0, tiled=True)
        return returned, down_add, up_add, both

    returned_parts = []
    grad_down = None
    grad_up = None
    previous = None
    for position in range(capacity):
        arrived = lax.all_to_all(
            send[:, position], "tok", split_axis=0, concat_axis=0, tiled=True
        )
        returned, down_add, up_add, previous = owner_part(arrived, previous)
        returned_parts.append(returned)
        grad_down = down_add if grad_down is None else grad_down + down_add
        grad_up = up_add if grad_up is None else grad_up + up_add
    grad_up = stored_scale[:, None, None] * grad_up
    returned = jnp.stack(returned_parts, axis=1).reshape(
        slots, BLOCK_TOKENS, width_portion + 2 * column_portion
    )
    mine = jnp.take(returned, destination, axis=0)

    base_out = lax.psum_scatter(
        lax.dot_general(
            frozen_weight, tokens, (((0,), (1,)), ((), ())), preferred_element_type=jnp.float32
        ),
        "tp",
        scatter_dimension=0,
        tiled=True,
    ).T
    increment = mine[:, :, width_portion : width_portion + column_portion].astype(
        jnp.float32
    ) + mine[:, :, width_portion + column_portion :].astype(jnp.float32)
    projected = (base_out + increment.reshape(token_rows, column_portion)).astype(jnp.bfloat16)
    token_gradient = mine[:, :, :width_portion].reshape(token_rows, width_portion)
    return (projected, token_gradient, grad_down, grad_up)


def solution(mesh):
    return jax.shard_map(
        per_device,
        mesh=mesh,
        in_specs=(
            P("tok", "tp"),
            P("tp", None),
            P("tok", "tp", None),
            P("tok", None, "tp"),
            P("tok"),
            P(),
            P(),
            P("tok", "tp"),
        ),
        out_specs=(P("tok", "tp"), P("tok", "tp"), P("tok", "tp", None), P("tok", None, "tp")),
        check_vma=False,
    )
```

```python
import jax
import jax.numpy as jnp
from jax import lax
from jax.sharding import PartitionSpec as P

ALPHA = 32
BLOCK_TOKENS = 16


def route(block_slot, number_adapters, capacity):
    owner_ids = block_slot // number_adapters
    block_ids = jnp.arange(block_slot.shape[-1], dtype=jnp.int32)
    earlier = (owner_ids[..., :, None] == owner_ids[..., None, :]) & (
        block_ids[None, :] < block_ids[:, None]
    )
    position = jnp.sum(earlier.astype(jnp.int32), axis=-1)
    return owner_ids * capacity + position


def tree_sum(value, axis):
    size = lax.axis_size(axis)
    step = 1
    while step < size:
        pairs = [(i, i ^ step) for i in range(size)]
        value = value + lax.ppermute(value, axis, pairs)
        step *= 2
    return value


def tree_gather(value, axis):
    size = lax.axis_size(axis)
    me = lax.axis_index(axis)
    value = value[None]
    step = 1
    while step < size:
        pairs = [(i, i ^ step) for i in range(size)]
        other = lax.ppermute(value, axis, pairs)
        low_side = (me & step) == 0
        value = jnp.where(
            low_side,
            jnp.concatenate([value, other], axis=0),
            jnp.concatenate([other, value], axis=0),
        )
        step *= 2
    return value


def split_pair(total):
    high = lax.reduce_precision(total, exponent_bits=8, mantissa_bits=7)
    return high.astype(jnp.bfloat16), (total - high).astype(jnp.bfloat16)


def tree_sum_gather(total, value, axis):
    size = lax.axis_size(axis)
    me = lax.axis_index(axis)
    rows, width = value.shape
    value = value[None]
    step = 1
    while step < size:
        pairs = [(i, i ^ step) for i in range(size)]
        high, low = split_pair(total)
        carried = jnp.concatenate([high, low], axis=1).reshape(1, rows, width)
        other = lax.ppermute(jnp.concatenate([value, carried], axis=0), axis, pairs)
        other_total = other[-1].reshape(rows, 2, width // 2)
        own = high.astype(jnp.float32) + low.astype(jnp.float32)
        total = own + (
            other_total[:, 0].astype(jnp.float32) + other_total[:, 1].astype(jnp.float32)
        )
        other = other[:-1]
        low_side = (me & step) == 0
        value = jnp.where(
            low_side,
            jnp.concatenate([value, other], axis=0),
            jnp.concatenate([other, value], axis=0),
        )
        step *= 2
    return total, value


def per_device(
    tokens,
    frozen_weight,
    adapter_down_matrices,
    adapter_up_matrices,
    adapter_per_block,
    slot_per_adapter,
    rank_per_adapter,
    output_gradient,
):
    tok_count = lax.axis_size("tok")
    tp_count = lax.axis_size("tp")
    me = lax.axis_index("tok")
    token_rows, width_portion = tokens.shape
    column_portion = output_gradient.shape[1]
    block_count = adapter_per_block.shape[0]
    number_adapters, _, rank_ceiling = adapter_down_matrices.shape
    capacity = max(2, 2 * block_count // tok_count)
    slots = tok_count * capacity
    row_total = slots * BLOCK_TOKENS
    lane = width_portion + column_portion

    block_slot = jnp.take(slot_per_adapter, adapter_per_block)
    destination = route(block_slot, number_adapters, capacity)
    local_index = block_slot % number_adapters
    slot_ids = jnp.arange(slots, dtype=jnp.int32)
    hit = destination[None, :] == slot_ids[:, None]
    filled = jnp.any(hit, axis=1)
    source_block = jnp.sum(
        jnp.where(hit, jnp.arange(block_count, dtype=jnp.int32)[None, :], 0), axis=1
    )
    tag = jnp.zeros((block_count, BLOCK_TOKENS, 128), jnp.bfloat16)
    tag = tag.at[:, 0, 0].set((local_index + 1).astype(jnp.bfloat16))
    packed = jnp.concatenate(
        [
            tokens.reshape(block_count, BLOCK_TOKENS, width_portion),
            output_gradient.reshape(block_count, BLOCK_TOKENS, column_portion),
            tag,
        ],
        axis=2,
    )
    send = jnp.where(filled[:, None, None], jnp.take(packed, source_block, axis=0), 0)
    send = send.reshape(tok_count, capacity, BLOCK_TOKENS, lane + 128)

    stored_ids = me * number_adapters + jnp.arange(number_adapters, dtype=jnp.int32)
    stored_match = slot_per_adapter[None, :] == stored_ids[:, None]
    stored_rank = jnp.sum(jnp.where(stored_match, rank_per_adapter[None, :], 0), axis=1)
    stored_scale = jnp.where(
        stored_rank > 0, jnp.float32(ALPHA) / jnp.maximum(stored_rank, 1).astype(jnp.float32), 0.0
    )
    part_rows = tok_count * BLOCK_TOKENS

    def owner_part(arrived, previous):
        slot_adapter = arrived[:, 0, lane].astype(jnp.int32) - 1
        input_rows = arrived[:, :, :width_portion].reshape(part_rows, width_portion)
        grad_rows = arrived[:, :, width_portion:lane].reshape(part_rows, column_portion)
        chosen = slot_adapter[:, None] == jnp.arange(number_adapters, dtype=jnp.int32)[None, :]
        chosen_rows = jnp.broadcast_to(
            chosen[:, None, :], (tok_count, BLOCK_TOKENS, number_adapters)
        ).reshape(part_rows, number_adapters)
        chosen_float = chosen_rows.astype(jnp.float32)
        row_rank = jnp.sum(jnp.where(chosen_rows, stored_rank[None, :], 0), axis=1)
        scale_per_row = jnp.sum(chosen_float * stored_scale[None, :], axis=1)
        keep_cols = jnp.arange(rank_ceiling, dtype=jnp.int32)[None, :] < row_rank[:, None]
        reduced_every_row = jnp.einsum(
            "ue,meb->umb", input_rows, adapter_down_matrices, preferred_element_type=jnp.float32
        )
        low_part = jnp.sum(reduced_every_row * chosen_float[:, :, None], axis=1)
        gathered_every_row = jnp.einsum(
            "hs,gbs->hgb", grad_rows, adapter_up_matrices, preferred_element_type=jnp.float32
        )
        pull_part = jnp.sum(gathered_every_row * chosen_float[:, :, None], axis=1)
        partial_sums = jnp.concatenate([low_part, pull_part], axis=1)
        if previous is not None:
            partial_sums, _ = lax.optimization_barrier((partial_sums, previous))
        both, every_column = tree_sum_gather(partial_sums, grad_rows, "tp")
        low_sum = both[:, :rank_ceiling]
        pull_sum = both[:, rank_ceiling:]
        reduced_rows = jnp.where(keep_cols, low_sum, 0.0).astype(jnp.bfloat16)
        reduced_gradient = (
            scale_per_row[:, None] * jnp.where(keep_cols, pull_sum, 0.0)
        ).astype(jnp.bfloat16)
        chosen_half = chosen_rows.astype(jnp.bfloat16)
        reduced_picked = chosen_half[:, :, None] * reduced_rows[:, None, :]
        gradient_picked = chosen_half[:, :, None] * reduced_gradient[:, None, :]
        adapter_increment = scale_per_row[:, None] * jnp.einsum(
            "hnq,nqs->hs", reduced_picked, adapter_up_matrices, preferred_element_type=jnp.float32
        )
        down_add = jnp.einsum(
            "rd,rak->adk", input_rows, gradient_picked, preferred_element_type=jnp.float32
        )
        up_add = jnp.einsum(
            "rak,rc->akc", reduced_picked, grad_rows, preferred_element_type=jnp.float32
        )
        adapter_output_rows = jnp.einsum(
            "ymf,mcf->yc", gradient_picked, adapter_down_matrices, preferred_element_type=jnp.float32
        )
        frozen_part = lax.dot_general(
            jnp.moveaxis(every_column, 0, 1).reshape(part_rows, tp_count * column_portion),
            frozen_weight,
            (((1,), (1,)), ((), ())),
            preferred_element_type=jnp.float32,
        )
        gradient_rows = (frozen_part + adapter_output_rows).astype(jnp.bfloat16)
        increment_round = lax.reduce_precision(adapter_increment, exponent_bits=8, mantissa_bits=7)
        increment_high = increment_round.astype(jnp.bfloat16)
        increment_low = (adapter_increment - increment_round).astype(jnp.bfloat16)
        back = jnp.concatenate(
            [
                gradient_rows.reshape(tok_count, BLOCK_TOKENS, width_portion),
                increment_high.reshape(tok_count, BLOCK_TOKENS, column_portion),
                increment_low.reshape(tok_count, BLOCK_TOKENS, column_portion),
            ],
            axis=2,
        )
        returned = lax.all_to_all(back, "tok", split_axis=0, concat_axis=0, tiled=True)
        return returned, down_add, up_add, both

    returned_parts = []
    grad_down = None
    grad_up = None
    previous = None
    for position in range(capacity):
        arrived = lax.all_to_all(
            send[:, position], "tok", split_axis=0, concat_axis=0, tiled=True
        )
        returned, down_add, up_add, previous = owner_part(arrived, previous)
        returned_parts.append(returned)
        grad_down = down_add if grad_down is None else grad_down + down_add
        grad_up = up_add if grad_up is None else grad_up + up_add
    grad_up = stored_scale[:, None, None] * grad_up
    returned = jnp.stack(returned_parts, axis=1).reshape(
        slots, BLOCK_TOKENS, width_portion + 2 * column_portion
    )
    mine = jnp.take(returned, destination, axis=0)

    base_out = lax.psum_scatter(
        lax.dot_general(
            frozen_weight, tokens, (((0,), (1,)), ((), ())), preferred_element_type=jnp.float32
        ),
        "tp",
        scatter_dimension=0,
        tiled=True,
    ).T
    increment = mine[:, :, width_portion : width_portion + column_portion].astype(
        jnp.float32
    ) + mine[:, :, width_portion + column_portion :].astype(jnp.float32)
    projected = (base_out + increment.reshape(token_rows, column_portion)).astype(jnp.bfloat16)
    token_gradient = mine[:, :, :width_portion].reshape(token_rows, width_portion)
    return (projected, token_gradient, grad_down, grad_up)


def solution(mesh):
    return jax.shard_map(
        per_device,
        mesh=mesh,
        in_specs=(
            P("tok", "tp"),
            P("tp", None),
            P("tok", "tp", None),
            P("tok", None, "tp"),
            P("tok"),
            P(),
            P(),
            P("tok", "tp"),
        ),
        out_specs=(P("tok", "tp"), P("tok", "tp"), P("tok", "tp", None), P("tok", None, "tp")),
        check_vma=False,
    )
```

```python
import jax
import jax.numpy as jnp
from jax import lax
from jax.sharding import PartitionSpec as P

ALPHA = 32
BLOCK_TOKENS = 16


def route(block_slot, number_adapters, capacity):
    owner_ids = block_slot // number_adapters
    block_ids = jnp.arange(block_slot.shape[-1], dtype=jnp.int32)
    earlier = (owner_ids[..., :, None] == owner_ids[..., None, :]) & (
        block_ids[None, :] < block_ids[:, None]
    )
    position = jnp.sum(earlier.astype(jnp.int32), axis=-1)
    return owner_ids * capacity + position


def tree_sum(value, axis):
    size = lax.axis_size(axis)
    step = 1
    while step < size:
        pairs = [(i, i ^ step) for i in range(size)]
        value = value + lax.ppermute(value, axis, pairs)
        step *= 2
    return value


def tree_gather(value, axis):
    size = lax.axis_size(axis)
    me = lax.axis_index(axis)
    value = value[None]
    step = 1
    while step < size:
        pairs = [(i, i ^ step) for i in range(size)]
        other = lax.ppermute(value, axis, pairs)
        low_side = (me & step) == 0
        value = jnp.where(
            low_side,
            jnp.concatenate([value, other], axis=0),
            jnp.concatenate([other, value], axis=0),
        )
        step *= 2
    return value


def split_pair(total):
    high = lax.reduce_precision(total, exponent_bits=8, mantissa_bits=7)
    return high.astype(jnp.bfloat16), (total - high).astype(jnp.bfloat16)


def tree_sum_gather(total, value, axis):
    size = lax.axis_size(axis)
    me = lax.axis_index(axis)
    rows, width = value.shape
    value = value[None]
    step = size // 2
    while step >= 1:
        pairs = [(i, i ^ step) for i in range(size)]
        high, low = split_pair(total)
        carried = jnp.concatenate([high, low], axis=1).reshape(1, rows, width)
        other = lax.ppermute(jnp.concatenate([value, carried], axis=0), axis, pairs)
        other_total = other[-1].reshape(rows, 2, width // 2)
        own = high.astype(jnp.float32) + low.astype(jnp.float32)
        total = own + (
            other_total[:, 0].astype(jnp.float32) + other_total[:, 1].astype(jnp.float32)
        )
        other = other[:-1]
        low_side = (me & step) == 0
        value = jnp.where(
            low_side,
            jnp.stack([value, other], axis=1),
            jnp.stack([other, value], axis=1),
        ).reshape(-1, rows, width)
        step //= 2
    return total, value


def per_device(
    tokens,
    frozen_weight,
    adapter_down_matrices,
    adapter_up_matrices,
    adapter_per_block,
    slot_per_adapter,
    rank_per_adapter,
    output_gradient,
):
    tok_count = lax.axis_size("tok")
    tp_count = lax.axis_size("tp")
    me = lax.axis_index("tok")
    token_rows, width_portion = tokens.shape
    column_portion = output_gradient.shape[1]
    block_count = adapter_per_block.shape[0]
    number_adapters, _, rank_ceiling = adapter_down_matrices.shape
    capacity = max(2, 2 * block_count // tok_count)
    slots = tok_count * capacity
    row_total = slots * BLOCK_TOKENS
    lane = width_portion + column_portion

    block_slot = jnp.take(slot_per_adapter, adapter_per_block)
    destination = route(block_slot, number_adapters, capacity)
    local_index = block_slot % number_adapters
    slot_ids = jnp.arange(slots, dtype=jnp.int32)
    hit = destination[None, :] == slot_ids[:, None]
    filled = jnp.any(hit, axis=1)
    source_block = jnp.sum(
        jnp.where(hit, jnp.arange(block_count, dtype=jnp.int32)[None, :], 0), axis=1
    )
    tag = jnp.zeros((block_count, BLOCK_TOKENS, 128), jnp.bfloat16)
    tag = tag.at[:, 0, 0].set((local_index + 1).astype(jnp.bfloat16))
    packed = jnp.concatenate(
        [
            tokens.reshape(block_count, BLOCK_TOKENS, width_portion),
            output_gradient.reshape(block_count, BLOCK_TOKENS, column_portion),
            tag,
        ],
        axis=2,
    )
    send = jnp.where(filled[:, None, None], jnp.take(packed, source_block, axis=0), 0)
    send = send.reshape(tok_count, capacity, BLOCK_TOKENS, lane + 128)

    stored_ids = me * number_adapters + jnp.arange(number_adapters, dtype=jnp.int32)
    stored_match = slot_per_adapter[None, :] == stored_ids[:, None]
    stored_rank = jnp.sum(jnp.where(stored_match, rank_per_adapter[None, :], 0), axis=1)
    stored_scale = jnp.where(
        stored_rank > 0, jnp.float32(ALPHA) / jnp.maximum(stored_rank, 1).astype(jnp.float32), 0.0
    )
    part_rows = tok_count * BLOCK_TOKENS

    def owner_part(arrived, previous):
        slot_adapter = arrived[:, 0, lane].astype(jnp.int32) - 1
        input_rows = arrived[:, :, :width_portion].reshape(part_rows, width_portion)
        grad_rows = arrived[:, :, width_portion:lane].reshape(part_rows, column_portion)
        chosen = slot_adapter[:, None] == jnp.arange(number_adapters, dtype=jnp.int32)[None, :]
        chosen_rows = jnp.broadcast_to(
            chosen[:, None, :], (tok_count, BLOCK_TOKENS, number_adapters)
        ).reshape(part_rows, number_adapters)
        chosen_float = chosen_rows.astype(jnp.float32)
        row_rank = jnp.sum(jnp.where(chosen_rows, stored_rank[None, :], 0), axis=1)
        scale_per_row = jnp.sum(chosen_float * stored_scale[None, :], axis=1)
        keep_cols = jnp.arange(rank_ceiling, dtype=jnp.int32)[None, :] < row_rank[:, None]
        reduced_every_row = jnp.einsum(
            "ue,meb->umb", input_rows, adapter_down_matrices, preferred_element_type=jnp.float32
        )
        low_part = jnp.sum(reduced_every_row * chosen_float[:, :, None], axis=1)
        gathered_every_row = jnp.einsum(
            "hs,gbs->hgb", grad_rows, adapter_up_matrices, preferred_element_type=jnp.float32
        )
        pull_part = jnp.sum(gathered_every_row * chosen_float[:, :, None], axis=1)
        partial_sums = jnp.concatenate([low_part, pull_part], axis=1)
        if previous is not None:
            partial_sums, _ = lax.optimization_barrier((partial_sums, previous))
        both, every_column = tree_sum_gather(partial_sums, grad_rows, "tp")
        low_sum = both[:, :rank_ceiling]
        pull_sum = both[:, rank_ceiling:]
        reduced_rows = jnp.where(keep_cols, low_sum, 0.0).astype(jnp.bfloat16)
        reduced_gradient = (
            scale_per_row[:, None] * jnp.where(keep_cols, pull_sum, 0.0)
        ).astype(jnp.bfloat16)
        chosen_half = chosen_rows.astype(jnp.bfloat16)
        reduced_picked = chosen_half[:, :, None] * reduced_rows[:, None, :]
        gradient_picked = chosen_half[:, :, None] * reduced_gradient[:, None, :]
        adapter_increment = scale_per_row[:, None] * jnp.einsum(
            "hnq,nqs->hs", reduced_picked, adapter_up_matrices, preferred_element_type=jnp.float32
        )
        down_add = jnp.einsum(
            "rd,rak->adk", input_rows, gradient_picked, preferred_element_type=jnp.float32
        )
        up_add = jnp.einsum(
            "rak,rc->akc", reduced_picked, grad_rows, preferred_element_type=jnp.float32
        )
        adapter_output_rows = jnp.einsum(
            "ymf,mcf->yc", gradient_picked, adapter_down_matrices, preferred_element_type=jnp.float32
        )
        frozen_part = lax.dot_general(
            jnp.moveaxis(every_column, 0, 1).reshape(part_rows, tp_count * column_portion),
            frozen_weight,
            (((1,), (1,)), ((), ())),
            preferred_element_type=jnp.float32,
        )
        gradient_rows = (frozen_part + adapter_output_rows).astype(jnp.bfloat16)
        increment_round = lax.reduce_precision(adapter_increment, exponent_bits=8, mantissa_bits=7)
        increment_high = increment_round.astype(jnp.bfloat16)
        increment_low = (adapter_increment - increment_round).astype(jnp.bfloat16)
        back = jnp.concatenate(
            [
                gradient_rows.reshape(tok_count, BLOCK_TOKENS, width_portion),
                increment_high.reshape(tok_count, BLOCK_TOKENS, column_portion),
                increment_low.reshape(tok_count, BLOCK_TOKENS, column_portion),
            ],
            axis=2,
        )
        returned = lax.all_to_all(back, "tok", split_axis=0, concat_axis=0, tiled=True)
        return returned, down_add, up_add, both

    returned_parts = []
    grad_down = None
    grad_up = None
    previous = None
    for position in range(capacity):
        arrived = lax.all_to_all(
            send[:, position], "tok", split_axis=0, concat_axis=0, tiled=True
        )
        returned, down_add, up_add, previous = owner_part(arrived, previous)
        returned_parts.append(returned)
        grad_down = down_add if grad_down is None else grad_down + down_add
        grad_up = up_add if grad_up is None else grad_up + up_add
    grad_up = stored_scale[:, None, None] * grad_up
    returned = jnp.stack(returned_parts, axis=1).reshape(
        slots, BLOCK_TOKENS, width_portion + 2 * column_portion
    )
    mine = jnp.take(returned, destination, axis=0)

    base_out = lax.psum_scatter(
        lax.dot_general(
            frozen_weight, tokens, (((0,), (1,)), ((), ())), preferred_element_type=jnp.float32
        ),
        "tp",
        scatter_dimension=0,
        tiled=True,
    ).T
    increment = mine[:, :, width_portion : width_portion + column_portion].astype(
        jnp.float32
    ) + mine[:, :, width_portion + column_portion :].astype(jnp.float32)
    projected = (base_out + increment.reshape(token_rows, column_portion)).astype(jnp.bfloat16)
    token_gradient = mine[:, :, :width_portion].reshape(token_rows, width_portion)
    return (projected, token_gradient, grad_down, grad_up)


def solution(mesh):
    return jax.shard_map(
        per_device,
        mesh=mesh,
        in_specs=(
            P("tok", "tp"),
            P("tp", None),
            P("tok", "tp", None),
            P("tok", None, "tp"),
            P("tok"),
            P(),
            P(),
            P("tok", "tp"),
        ),
        out_specs=(P("tok", "tp"), P("tok", "tp"), P("tok", "tp", None), P("tok", None, "tp")),
        check_vma=False,
    )
```

```python
import jax
import jax.numpy as jnp
from jax import lax
from jax.sharding import PartitionSpec as P

ALPHA = 32
BLOCK_TOKENS = 16


def route(block_slot, number_adapters, capacity):
    owner_ids = block_slot // number_adapters
    block_ids = jnp.arange(block_slot.shape[-1], dtype=jnp.int32)
    earlier = (owner_ids[..., :, None] == owner_ids[..., None, :]) & (
        block_ids[None, :] < block_ids[:, None]
    )
    position = jnp.sum(earlier.astype(jnp.int32), axis=-1)
    return owner_ids * capacity + position


def tree_sum(value, axis):
    size = lax.axis_size(axis)
    step = 1
    while step < size:
        pairs = [(i, i ^ step) for i in range(size)]
        value = value + lax.ppermute(value, axis, pairs)
        step *= 2
    return value


def tree_gather(value, axis):
    size = lax.axis_size(axis)
    me = lax.axis_index(axis)
    value = value[None]
    step = 1
    while step < size:
        pairs = [(i, i ^ step) for i in range(size)]
        other = lax.ppermute(value, axis, pairs)
        low_side = (me & step) == 0
        value = jnp.where(
            low_side,
            jnp.concatenate([value, other], axis=0),
            jnp.concatenate([other, value], axis=0),
        )
        step *= 2
    return value


def split_pair(total):
    high = lax.reduce_precision(total, exponent_bits=8, mantissa_bits=7)
    return high.astype(jnp.bfloat16), (total - high).astype(jnp.bfloat16)


def tree_sum_gather(total, value, axis):
    size = lax.axis_size(axis)
    me = lax.axis_index(axis)
    rows, width = value.shape
    value = value[None]
    step = size // 2
    while step >= 1:
        pairs = [(i, i ^ step) for i in range(size)]
        high, low = split_pair(total)
        carried = jnp.concatenate([high, low], axis=1).reshape(1, rows, width)
        other = lax.ppermute(jnp.concatenate([value, carried], axis=0), axis, pairs)
        other_total = other[-1].reshape(rows, 2, width // 2)
        own = high.astype(jnp.float32) + low.astype(jnp.float32)
        total = own + (
            other_total[:, 0].astype(jnp.float32) + other_total[:, 1].astype(jnp.float32)
        )
        other = other[:-1]
        low_side = (me & step) == 0
        value = jnp.where(
            low_side,
            jnp.stack([value, other], axis=1),
            jnp.stack([other, value], axis=1),
        ).reshape(-1, rows, width)
        step //= 2
    return total, value


def per_device(
    tokens,
    frozen_weight,
    adapter_down_matrices,
    adapter_up_matrices,
    adapter_per_block,
    slot_per_adapter,
    rank_per_adapter,
    output_gradient,
):
    tok_count = lax.axis_size("tok")
    tp_count = lax.axis_size("tp")
    me = lax.axis_index("tok")
    token_rows, width_portion = tokens.shape
    column_portion = output_gradient.shape[1]
    block_count = adapter_per_block.shape[0]
    number_adapters, _, rank_ceiling = adapter_down_matrices.shape
    capacity = max(2, 2 * block_count // tok_count)
    slots = tok_count * capacity
    row_total = slots * BLOCK_TOKENS
    lane = width_portion + column_portion

    block_slot = jnp.take(slot_per_adapter, adapter_per_block)
    destination = route(block_slot, number_adapters, capacity)
    local_index = block_slot % number_adapters
    slot_ids = jnp.arange(slots, dtype=jnp.int32)
    hit = destination[None, :] == slot_ids[:, None]
    filled = jnp.any(hit, axis=1)
    source_block = jnp.sum(
        jnp.where(hit, jnp.arange(block_count, dtype=jnp.int32)[None, :], 0), axis=1
    )
    tag = jnp.zeros((block_count, BLOCK_TOKENS, 128), jnp.bfloat16)
    tag = tag.at[:, 0, 0].set((local_index + 1).astype(jnp.bfloat16))
    packed = jnp.concatenate(
        [
            tokens.reshape(block_count, BLOCK_TOKENS, width_portion),
            output_gradient.reshape(block_count, BLOCK_TOKENS, column_portion),
            tag,
        ],
        axis=2,
    )
    send = jnp.where(filled[:, None, None], jnp.take(packed, source_block, axis=0), 0)
    send = send.reshape(tok_count, capacity, BLOCK_TOKENS, lane + 128)

    stored_ids = me * number_adapters + jnp.arange(number_adapters, dtype=jnp.int32)
    stored_match = slot_per_adapter[None, :] == stored_ids[:, None]
    stored_rank = jnp.sum(jnp.where(stored_match, rank_per_adapter[None, :], 0), axis=1)
    stored_scale = jnp.where(
        stored_rank > 0, jnp.float32(ALPHA) / jnp.maximum(stored_rank, 1).astype(jnp.float32), 0.0
    )
    def owner_part(arrived, previous):
        part_slots = arrived.shape[0]
        part_rows = part_slots * BLOCK_TOKENS
        slot_adapter = arrived[:, 0, lane].astype(jnp.int32) - 1
        input_rows = arrived[:, :, :width_portion].reshape(part_rows, width_portion)
        grad_rows = arrived[:, :, width_portion:lane].reshape(part_rows, column_portion)
        chosen = slot_adapter[:, None] == jnp.arange(number_adapters, dtype=jnp.int32)[None, :]
        chosen_rows = jnp.broadcast_to(
            chosen[:, None, :], (part_slots, BLOCK_TOKENS, number_adapters)
        ).reshape(part_rows, number_adapters)
        chosen_float = chosen_rows.astype(jnp.float32)
        row_rank = jnp.sum(jnp.where(chosen_rows, stored_rank[None, :], 0), axis=1)
        scale_per_row = jnp.sum(chosen_float * stored_scale[None, :], axis=1)
        keep_cols = jnp.arange(rank_ceiling, dtype=jnp.int32)[None, :] < row_rank[:, None]
        reduced_every_row = jnp.einsum(
            "ue,meb->umb", input_rows, adapter_down_matrices, preferred_element_type=jnp.float32
        )
        low_part = jnp.sum(reduced_every_row * chosen_float[:, :, None], axis=1)
        gathered_every_row = jnp.einsum(
            "hs,gbs->hgb", grad_rows, adapter_up_matrices, preferred_element_type=jnp.float32
        )
        pull_part = jnp.sum(gathered_every_row * chosen_float[:, :, None], axis=1)
        partial_sums = jnp.concatenate([low_part, pull_part], axis=1)
        if previous is not None:
            partial_sums, _ = lax.optimization_barrier((partial_sums, previous))
        both, every_column = tree_sum_gather(partial_sums, grad_rows, "tp")
        low_sum = both[:, :rank_ceiling]
        pull_sum = both[:, rank_ceiling:]
        reduced_rows = jnp.where(keep_cols, low_sum, 0.0).astype(jnp.bfloat16)
        reduced_gradient = (
            scale_per_row[:, None] * jnp.where(keep_cols, pull_sum, 0.0)
        ).astype(jnp.bfloat16)
        chosen_half = chosen_rows.astype(jnp.bfloat16)
        reduced_picked = chosen_half[:, :, None] * reduced_rows[:, None, :]
        gradient_picked = chosen_half[:, :, None] * reduced_gradient[:, None, :]
        adapter_increment = scale_per_row[:, None] * jnp.einsum(
            "hnq,nqs->hs", reduced_picked, adapter_up_matrices, preferred_element_type=jnp.float32
        )
        down_add = jnp.einsum(
            "rd,rak->adk", input_rows, gradient_picked, preferred_element_type=jnp.float32
        )
        up_add = jnp.einsum(
            "rak,rc->akc", reduced_picked, grad_rows, preferred_element_type=jnp.float32
        )
        adapter_output_rows = jnp.einsum(
            "ymf,mcf->yc", gradient_picked, adapter_down_matrices, preferred_element_type=jnp.float32
        )
        frozen_part = lax.dot_general(
            jnp.moveaxis(every_column, 0, 1).reshape(part_rows, tp_count * column_portion),
            frozen_weight,
            (((1,), (1,)), ((), ())),
            preferred_element_type=jnp.float32,
        )
        gradient_rows = (frozen_part + adapter_output_rows).astype(jnp.bfloat16)
        increment_round = lax.reduce_precision(adapter_increment, exponent_bits=8, mantissa_bits=7)
        increment_high = increment_round.astype(jnp.bfloat16)
        increment_low = (adapter_increment - increment_round).astype(jnp.bfloat16)
        back = jnp.concatenate(
            [
                gradient_rows.reshape(part_slots, BLOCK_TOKENS, width_portion),
                increment_high.reshape(part_slots, BLOCK_TOKENS, column_portion),
                increment_low.reshape(part_slots, BLOCK_TOKENS, column_portion),
            ],
            axis=2,
        )
        returned = lax.all_to_all(back, "tok", split_axis=0, concat_axis=0, tiled=True)
        return returned, down_add, up_add, both

    arrived = lax.all_to_all(send, "tok", split_axis=0, concat_axis=0, tiled=True)
    returned, grad_down, grad_up, _ = owner_part(
        arrived.reshape(slots, BLOCK_TOKENS, lane + 128), None
    )
    grad_up = stored_scale[:, None, None] * grad_up
    mine = jnp.take(returned, destination, axis=0)

    base_out = lax.psum_scatter(
        lax.dot_general(
            frozen_weight, tokens, (((0,), (1,)), ((), ())), preferred_element_type=jnp.float32
        ),
        "tp",
        scatter_dimension=0,
        tiled=True,
    ).T
    increment = mine[:, :, width_portion : width_portion + column_portion].astype(
        jnp.float32
    ) + mine[:, :, width_portion + column_portion :].astype(jnp.float32)
    projected = (base_out + increment.reshape(token_rows, column_portion)).astype(jnp.bfloat16)
    token_gradient = mine[:, :, :width_portion].reshape(token_rows, width_portion)
    return (projected, token_gradient, grad_down, grad_up)


def solution(mesh):
    return jax.shard_map(
        per_device,
        mesh=mesh,
        in_specs=(
            P("tok", "tp"),
            P("tp", None),
            P("tok", "tp", None),
            P("tok", None, "tp"),
            P("tok"),
            P(),
            P(),
            P("tok", "tp"),
        ),
        out_specs=(P("tok", "tp"), P("tok", "tp"), P("tok", "tp", None), P("tok", None, "tp")),
        check_vma=False,
    )
```

```python
import jax
import jax.numpy as jnp
from jax import lax
from jax.sharding import PartitionSpec as P

ALPHA = 32
BLOCK_TOKENS = 16


def per_device(
    tokens,
    frozen_weight,
    adapter_down_matrices,
    adapter_up_matrices,
    adapter_per_block,
    slot_per_adapter,
    rank_per_adapter,
    output_gradient,
):
    tok_count = lax.axis_size("tok")
    token_rows = tokens.shape[0]
    width_portion = tokens.shape[1]
    column_portion = output_gradient.shape[1]
    block_count = adapter_per_block.shape[0]
    number_adapters = adapter_down_matrices.shape[0]
    rank_ceiling = adapter_down_matrices.shape[2]
    capacity = max(2, 2 * block_count // tok_count)
    storage_position_count = tok_count * capacity
    adapter_total = slot_per_adapter.shape[0]
    weight_cols = frozen_weight
    base_out = lax.psum_scatter(
        lax.dot_general(
            weight_cols, tokens, (((0,), (1,)), ((), ())), preferred_element_type=jnp.float32
        ),
        "tp",
        scatter_dimension=0,
        tiled=True,
    ).T
    adapter_ids = jnp.arange(adapter_total, dtype=jnp.int32)
    matches = adapter_per_block[:, None] == adapter_ids[None, :]
    block_slot = jnp.sum(jnp.where(matches, slot_per_adapter[None, :], 0), axis=1)
    owner_ids = block_slot // number_adapters
    local_index = block_slot % number_adapters
    block_ids = jnp.arange(block_count, dtype=jnp.int32)
    earlier = (owner_ids[:, None] == owner_ids[None, :]) & (block_ids[None, :] < block_ids[:, None])
    position = jnp.sum(earlier.astype(jnp.int32), axis=1)
    destination = owner_ids * capacity + position
    placement = jnp.arange(storage_position_count, dtype=jnp.int32)[:, None] == destination[None, :]
    place_matrix = placement.astype(jnp.bfloat16)
    send_rows = jnp.dot(
        place_matrix,
        tokens.reshape(block_count, BLOCK_TOKENS * width_portion),
        preferred_element_type=jnp.float32,
    ).astype(jnp.bfloat16)
    send_grads = jnp.dot(
        place_matrix,
        output_gradient.reshape(block_count, BLOCK_TOKENS * column_portion),
        preferred_element_type=jnp.float32,
    ).astype(jnp.bfloat16)
    slot_adapter = jnp.sum(jnp.where(placement, local_index[None, :] + 1, 0), axis=1) - 1
    tag = jnp.zeros((storage_position_count, BLOCK_TOKENS, 128), jnp.bfloat16)
    tag = tag.at[:, 0, 0].set((slot_adapter + 1).astype(jnp.bfloat16))
    tagged_grads = jnp.concatenate(
        [send_grads.reshape(storage_position_count, BLOCK_TOKENS, column_portion), tag], axis=2
    )
    arrived_rows, arrived_tagged = (
        lax.all_to_all(
            send_rows.reshape(storage_position_count, BLOCK_TOKENS, width_portion),
            "tok",
            split_axis=0,
            concat_axis=0,
            tiled=True,
        ),
        lax.all_to_all(tagged_grads, "tok", split_axis=0, concat_axis=0, tiled=True),
    )
    arrived_grads = arrived_tagged[:, :, :column_portion]
    arrived_adapter = arrived_tagged[:, 0, column_portion].astype(jnp.int32) - 1
    row_total = storage_position_count * BLOCK_TOKENS
    input_row_block = arrived_rows.reshape(row_total, width_portion)
    gradient_row_block = arrived_grads.reshape(row_total, column_portion)
    chosen = arrived_adapter[:, None] == jnp.arange(number_adapters, dtype=jnp.int32)[None, :]
    chosen_rows = jnp.broadcast_to(
        chosen[:, None, :], (storage_position_count, BLOCK_TOKENS, number_adapters)
    ).reshape(row_total, number_adapters)
    chosen_float = chosen_rows.astype(jnp.float32)
    chosen_half = chosen_rows.astype(jnp.bfloat16)
    stored_ids = lax.axis_index("tok") * number_adapters + jnp.arange(
        number_adapters, dtype=jnp.int32
    )
    stored_match = slot_per_adapter[None, :] == stored_ids[:, None]
    stored_rank = jnp.sum(jnp.where(stored_match, rank_per_adapter[None, :], 0), axis=1)
    stored_scale = jnp.where(
        stored_rank > 0, jnp.float32(ALPHA) / jnp.maximum(stored_rank, 1).astype(jnp.float32), 0.0
    )
    row_rank = jnp.sum(jnp.where(chosen_rows, stored_rank[None, :], 0), axis=1)
    scale_per_row = jnp.sum(chosen_float * stored_scale[None, :], axis=1)
    keep_cols = jnp.arange(rank_ceiling, dtype=jnp.int32)[None, :] < row_rank[:, None]
    reduced_every_row = jnp.einsum(
        "ue,meb->umb", input_row_block, adapter_down_matrices, preferred_element_type=jnp.float32
    )
    low_part = jnp.sum(reduced_every_row * chosen_float[:, :, None], axis=1)
    gathered_every_row = jnp.einsum(
        "hs,gbs->hgb", gradient_row_block, adapter_up_matrices, preferred_element_type=jnp.float32
    )
    pull_part = jnp.sum(gathered_every_row * chosen_float[:, :, None], axis=1)
    low_sum, pull_sum = lax.psum((low_part, pull_part), "tp")
    reduced_rows = jnp.where(keep_cols, low_sum, 0.0).astype(jnp.bfloat16)
    reduced_gradient = (scale_per_row[:, None] * jnp.where(keep_cols, pull_sum, 0.0)).astype(
        jnp.bfloat16
    )
    reduced_picked = chosen_half[:, :, None] * reduced_rows[:, None, :]
    gradient_picked = chosen_half[:, :, None] * reduced_gradient[:, None, :]
    adapter_increment = scale_per_row[:, None] * jnp.einsum(
        "hnq,nqs->hs", reduced_picked, adapter_up_matrices, preferred_element_type=jnp.float32
    )
    grad_down = jnp.einsum(
        "rd,rak->adk", input_row_block, gradient_picked, preferred_element_type=jnp.float32
    )
    grad_up = stored_scale[:, None, None] * jnp.einsum(
        "rak,rc->akc", reduced_picked, gradient_row_block, preferred_element_type=jnp.float32
    )
    adapter_output_rows = jnp.einsum(
        "ymf,mcf->yc", gradient_picked, adapter_down_matrices, preferred_element_type=jnp.float32
    )
    returned = lax.all_to_all(
        jnp.concatenate(
            [
                adapter_output_rows.reshape(storage_position_count, BLOCK_TOKENS, width_portion),
                adapter_increment.reshape(storage_position_count, BLOCK_TOKENS, column_portion),
            ],
            axis=2,
        ),
        "tok",
        split_axis=0,
        concat_axis=0,
        tiled=True,
    )
    row_input_gradient = returned[:, :, :width_portion]
    delta_back = returned[:, :, width_portion:]
    adapter_input_gradient = jnp.take(row_input_gradient, destination, axis=0)
    mine_delta = jnp.take(delta_back, destination, axis=0)
    projected = (base_out + mine_delta.reshape(token_rows, column_portion)).astype(jnp.bfloat16)
    weight_cols = frozen_weight
    frozen_input_gradient = lax.dot_general(
        lax.all_gather(output_gradient, "tp", axis=1, tiled=True),
        weight_cols,
        (((1,), (1,)), ((), ())),
        preferred_element_type=jnp.float32,
    )
    token_gradient = (
        frozen_input_gradient + adapter_input_gradient.reshape(token_rows, width_portion)
    ).astype(jnp.bfloat16)
    return (projected, token_gradient, grad_down, grad_up)


def solution(mesh):
    return jax.shard_map(
        per_device,
        mesh=mesh,
        in_specs=(
            P("tok", "tp"),
            P("tp", None),
            P("tok", "tp", None),
            P("tok", None, "tp"),
            P("tok"),
            P(),
            P(),
            P("tok", "tp"),
        ),
        out_specs=(P("tok", "tp"), P("tok", "tp"), P("tok", "tp", None), P("tok", None, "tp")),
        check_vma=False,
    )
```

```python
import jax
import jax.numpy as jnp
from jax import lax
from jax.sharding import PartitionSpec as P

ALPHA = 32
BLOCK_TOKENS = 16


def per_device(
    tokens,
    frozen_weight,
    adapter_down_matrices,
    adapter_up_matrices,
    adapter_per_block,
    slot_per_adapter,
    rank_per_adapter,
    output_gradient,
):
    tok_count = lax.axis_size("tok")
    token_rows = tokens.shape[0]
    width_portion = tokens.shape[1]
    column_portion = output_gradient.shape[1]
    block_count = adapter_per_block.shape[0]
    number_adapters = adapter_down_matrices.shape[0]
    rank_ceiling = adapter_down_matrices.shape[2]
    capacity = max(2, 2 * block_count // tok_count)
    storage_position_count = tok_count * capacity
    adapter_total = slot_per_adapter.shape[0]
    weight_cols = frozen_weight
    base_out = lax.psum_scatter(
        lax.dot_general(
            weight_cols, tokens, (((0,), (1,)), ((), ())), preferred_element_type=jnp.float32
        ),
        "tp",
        scatter_dimension=0,
        tiled=True,
    ).T
    adapter_ids = jnp.arange(adapter_total, dtype=jnp.int32)
    matches = adapter_per_block[:, None] == adapter_ids[None, :]
    block_slot = jnp.sum(jnp.where(matches, slot_per_adapter[None, :], 0), axis=1)
    owner_ids = block_slot // number_adapters
    local_index = block_slot % number_adapters
    block_ids = jnp.arange(block_count, dtype=jnp.int32)
    earlier = (owner_ids[:, None] == owner_ids[None, :]) & (block_ids[None, :] < block_ids[:, None])
    position = jnp.sum(earlier.astype(jnp.int32), axis=1)
    destination = owner_ids * capacity + position
    placement = jnp.arange(storage_position_count, dtype=jnp.int32)[:, None] == destination[None, :]
    place_matrix = placement.astype(jnp.bfloat16)
    send_rows = jnp.dot(
        place_matrix,
        tokens.reshape(block_count, BLOCK_TOKENS * width_portion),
        preferred_element_type=jnp.float32,
    ).astype(jnp.bfloat16)
    send_grads = jnp.dot(
        place_matrix,
        output_gradient.reshape(block_count, BLOCK_TOKENS * column_portion),
        preferred_element_type=jnp.float32,
    ).astype(jnp.bfloat16)
    slot_adapter = jnp.sum(jnp.where(placement, local_index[None, :] + 1, 0), axis=1) - 1
    tag = jnp.zeros((storage_position_count, BLOCK_TOKENS, 128), jnp.bfloat16)
    tag = tag.at[:, 0, 0].set((slot_adapter + 1).astype(jnp.bfloat16))
    tagged_grads = jnp.concatenate(
        [send_grads.reshape(storage_position_count, BLOCK_TOKENS, column_portion), tag], axis=2
    )
    arrived_tagged = lax.all_to_all(tagged_grads, "tok", split_axis=0, concat_axis=0, tiled=True)
    send_rows, arrived_tagged = lax.optimization_barrier((send_rows, arrived_tagged))
    arrived_rows = lax.all_to_all(
        send_rows.reshape(storage_position_count, BLOCK_TOKENS, width_portion),
        "tok",
        split_axis=0,
        concat_axis=0,
        tiled=True,
    )
    arrived_grads = arrived_tagged[:, :, :column_portion]
    arrived_adapter = arrived_tagged[:, 0, column_portion].astype(jnp.int32) - 1
    row_total = storage_position_count * BLOCK_TOKENS
    input_row_block = arrived_rows.reshape(row_total, width_portion)
    gradient_row_block = arrived_grads.reshape(row_total, column_portion)
    chosen = arrived_adapter[:, None] == jnp.arange(number_adapters, dtype=jnp.int32)[None, :]
    chosen_rows = jnp.broadcast_to(
        chosen[:, None, :], (storage_position_count, BLOCK_TOKENS, number_adapters)
    ).reshape(row_total, number_adapters)
    chosen_float = chosen_rows.astype(jnp.float32)
    chosen_half = chosen_rows.astype(jnp.bfloat16)
    stored_ids = lax.axis_index("tok") * number_adapters + jnp.arange(
        number_adapters, dtype=jnp.int32
    )
    stored_match = slot_per_adapter[None, :] == stored_ids[:, None]
    stored_rank = jnp.sum(jnp.where(stored_match, rank_per_adapter[None, :], 0), axis=1)
    stored_scale = jnp.where(
        stored_rank > 0, jnp.float32(ALPHA) / jnp.maximum(stored_rank, 1).astype(jnp.float32), 0.0
    )
    row_rank = jnp.sum(jnp.where(chosen_rows, stored_rank[None, :], 0), axis=1)
    scale_per_row = jnp.sum(chosen_float * stored_scale[None, :], axis=1)
    keep_cols = jnp.arange(rank_ceiling, dtype=jnp.int32)[None, :] < row_rank[:, None]
    reduced_every_row = jnp.einsum(
        "ue,meb->umb", input_row_block, adapter_down_matrices, preferred_element_type=jnp.float32
    )
    low_part = jnp.sum(reduced_every_row * chosen_float[:, :, None], axis=1)
    gathered_every_row = jnp.einsum(
        "hs,gbs->hgb", gradient_row_block, adapter_up_matrices, preferred_element_type=jnp.float32
    )
    pull_part = jnp.sum(gathered_every_row * chosen_float[:, :, None], axis=1)
    low_sum, pull_sum = lax.psum((low_part, pull_part), "tp")
    reduced_rows = jnp.where(keep_cols, low_sum, 0.0).astype(jnp.bfloat16)
    reduced_gradient = (scale_per_row[:, None] * jnp.where(keep_cols, pull_sum, 0.0)).astype(
        jnp.bfloat16
    )
    reduced_picked = chosen_half[:, :, None] * reduced_rows[:, None, :]
    gradient_picked = chosen_half[:, :, None] * reduced_gradient[:, None, :]
    adapter_increment = scale_per_row[:, None] * jnp.einsum(
        "hnq,nqs->hs", reduced_picked, adapter_up_matrices, preferred_element_type=jnp.float32
    )
    grad_down = jnp.einsum(
        "rd,rak->adk", input_row_block, gradient_picked, preferred_element_type=jnp.float32
    )
    grad_up = stored_scale[:, None, None] * jnp.einsum(
        "rak,rc->akc", reduced_picked, gradient_row_block, preferred_element_type=jnp.float32
    )
    adapter_output_rows = jnp.einsum(
        "ymf,mcf->yc", gradient_picked, adapter_down_matrices, preferred_element_type=jnp.float32
    )
    returned = lax.all_to_all(
        jnp.concatenate(
            [
                adapter_output_rows.reshape(storage_position_count, BLOCK_TOKENS, width_portion),
                adapter_increment.reshape(storage_position_count, BLOCK_TOKENS, column_portion),
            ],
            axis=2,
        ),
        "tok",
        split_axis=0,
        concat_axis=0,
        tiled=True,
    )
    row_input_gradient = returned[:, :, :width_portion]
    delta_back = returned[:, :, width_portion:]
    adapter_input_gradient = jnp.take(row_input_gradient, destination, axis=0)
    mine_delta = jnp.take(delta_back, destination, axis=0)
    projected = (base_out + mine_delta.reshape(token_rows, column_portion)).astype(jnp.bfloat16)
    weight_cols = frozen_weight
    frozen_input_gradient = lax.dot_general(
        lax.all_gather(output_gradient, "tp", axis=1, tiled=True),
        weight_cols,
        (((1,), (1,)), ((), ())),
        preferred_element_type=jnp.float32,
    )
    token_gradient = (
        frozen_input_gradient + adapter_input_gradient.reshape(token_rows, width_portion)
    ).astype(jnp.bfloat16)
    return (projected, token_gradient, grad_down, grad_up)


def solution(mesh):
    return jax.shard_map(
        per_device,
        mesh=mesh,
        in_specs=(
            P("tok", "tp"),
            P("tp", None),
            P("tok", "tp", None),
            P("tok", None, "tp"),
            P("tok"),
            P(),
            P(),
            P("tok", "tp"),
        ),
        out_specs=(P("tok", "tp"), P("tok", "tp"), P("tok", "tp", None), P("tok", None, "tp")),
        check_vma=False,
    )
```

```python
import jax
import jax.numpy as jnp
from jax import lax
from jax.sharding import PartitionSpec as P

ALPHA = 32
BLOCK_TOKENS = 16


def per_device(
    tokens,
    frozen_weight,
    adapter_down_matrices,
    adapter_up_matrices,
    adapter_per_block,
    slot_per_adapter,
    rank_per_adapter,
    output_gradient,
):
    tok_count = lax.axis_size("tok")
    token_rows = tokens.shape[0]
    width_portion = tokens.shape[1]
    column_portion = output_gradient.shape[1]
    block_count = adapter_per_block.shape[0]
    number_adapters = adapter_down_matrices.shape[0]
    rank_ceiling = adapter_down_matrices.shape[2]
    capacity = max(2, 2 * block_count // tok_count)
    storage_position_count = tok_count * capacity
    adapter_total = slot_per_adapter.shape[0]
    weight_cols = frozen_weight
    base_out = lax.psum_scatter(
        lax.dot_general(
            weight_cols, tokens, (((0,), (1,)), ((), ())), preferred_element_type=jnp.float32
        ),
        "tp",
        scatter_dimension=0,
        tiled=True,
    ).T
    adapter_ids = jnp.arange(adapter_total, dtype=jnp.int32)
    matches = adapter_per_block[:, None] == adapter_ids[None, :]
    block_slot = jnp.sum(jnp.where(matches, slot_per_adapter[None, :], 0), axis=1)
    owner_ids = block_slot // number_adapters
    local_index = block_slot % number_adapters
    block_ids = jnp.arange(block_count, dtype=jnp.int32)
    earlier = (owner_ids[:, None] == owner_ids[None, :]) & (block_ids[None, :] < block_ids[:, None])
    position = jnp.sum(earlier.astype(jnp.int32), axis=1)
    destination = owner_ids * capacity + position
    placement = jnp.arange(storage_position_count, dtype=jnp.int32)[:, None] == destination[None, :]
    place_matrix = placement.astype(jnp.bfloat16)
    send_rows = jnp.dot(
        place_matrix,
        tokens.reshape(block_count, BLOCK_TOKENS * width_portion),
        preferred_element_type=jnp.float32,
    ).astype(jnp.bfloat16)
    send_grads = jnp.dot(
        place_matrix,
        output_gradient.reshape(block_count, BLOCK_TOKENS * column_portion),
        preferred_element_type=jnp.float32,
    ).astype(jnp.bfloat16)
    slot_adapter = jnp.sum(jnp.where(placement, local_index[None, :] + 1, 0), axis=1) - 1
    arrived_rows, arrived_grads, arrived_adapter = (
        lax.all_to_all(
            send_rows.reshape(storage_position_count, BLOCK_TOKENS, width_portion),
            "tok",
            split_axis=0,
            concat_axis=0,
            tiled=True,
        ),
        lax.all_to_all(
            send_grads.reshape(storage_position_count, BLOCK_TOKENS, column_portion),
            "tok",
            split_axis=0,
            concat_axis=0,
            tiled=True,
        ),
        lax.all_to_all(slot_adapter, "tok", split_axis=0, concat_axis=0, tiled=True),
    )
    row_total = storage_position_count * BLOCK_TOKENS
    input_row_block = arrived_rows.reshape(row_total, width_portion)
    gradient_row_block = arrived_grads.reshape(row_total, column_portion)
    chosen = arrived_adapter[:, None] == jnp.arange(number_adapters, dtype=jnp.int32)[None, :]
    chosen_rows = jnp.broadcast_to(
        chosen[:, None, :], (storage_position_count, BLOCK_TOKENS, number_adapters)
    ).reshape(row_total, number_adapters)
    chosen_float = chosen_rows.astype(jnp.float32)
    chosen_half = chosen_rows.astype(jnp.bfloat16)
    stored_ids = lax.axis_index("tok") * number_adapters + jnp.arange(
        number_adapters, dtype=jnp.int32
    )
    stored_match = slot_per_adapter[None, :] == stored_ids[:, None]
    stored_rank = jnp.sum(jnp.where(stored_match, rank_per_adapter[None, :], 0), axis=1)
    stored_scale = jnp.where(
        stored_rank > 0, jnp.float32(ALPHA) / jnp.maximum(stored_rank, 1).astype(jnp.float32), 0.0
    )
    row_rank = jnp.sum(jnp.where(chosen_rows, stored_rank[None, :], 0), axis=1)
    scale_per_row = jnp.sum(chosen_float * stored_scale[None, :], axis=1)
    keep_cols = jnp.arange(rank_ceiling, dtype=jnp.int32)[None, :] < row_rank[:, None]
    reduced_every_row = jnp.einsum(
        "ue,meb->umb", input_row_block, adapter_down_matrices, preferred_element_type=jnp.float32
    )
    low_part = jnp.sum(reduced_every_row * chosen_float[:, :, None], axis=1)
    gathered_every_row = jnp.einsum(
        "hs,gbs->hgb", gradient_row_block, adapter_up_matrices, preferred_element_type=jnp.float32
    )
    pull_part = jnp.sum(gathered_every_row * chosen_float[:, :, None], axis=1)
    low_sum, pull_sum = lax.psum((low_part, pull_part), "tp")
    reduced_rows = jnp.where(keep_cols, low_sum, 0.0).astype(jnp.bfloat16)
    reduced_gradient = (scale_per_row[:, None] * jnp.where(keep_cols, pull_sum, 0.0)).astype(
        jnp.bfloat16
    )
    reduced_picked = chosen_half[:, :, None] * reduced_rows[:, None, :]
    gradient_picked = chosen_half[:, :, None] * reduced_gradient[:, None, :]
    adapter_increment = scale_per_row[:, None] * jnp.einsum(
        "hnq,nqs->hs", reduced_picked, adapter_up_matrices, preferred_element_type=jnp.float32
    )
    grad_down = jnp.einsum(
        "rd,rak->adk", input_row_block, gradient_picked, preferred_element_type=jnp.float32
    )
    grad_up = stored_scale[:, None, None] * jnp.einsum(
        "rak,rc->akc", reduced_picked, gradient_row_block, preferred_element_type=jnp.float32
    )
    adapter_output_rows = jnp.einsum(
        "ymf,mcf->yc", gradient_picked, adapter_down_matrices, preferred_element_type=jnp.float32
    )
    returned = lax.all_to_all(
        jnp.concatenate(
            [
                adapter_output_rows.reshape(storage_position_count, BLOCK_TOKENS, width_portion),
                adapter_increment.reshape(storage_position_count, BLOCK_TOKENS, column_portion),
            ],
            axis=2,
        ),
        "tok",
        split_axis=0,
        concat_axis=0,
        tiled=True,
    )
    row_input_gradient = returned[:, :, :width_portion]
    delta_back = returned[:, :, width_portion:]
    adapter_input_gradient = jnp.take(row_input_gradient, destination, axis=0)
    mine_delta = jnp.take(delta_back, destination, axis=0)
    projected = (base_out + mine_delta.reshape(token_rows, column_portion)).astype(jnp.bfloat16)
    weight_cols = frozen_weight
    frozen_input_gradient = lax.dot_general(
        lax.all_gather(output_gradient, "tp", axis=1, tiled=True),
        weight_cols,
        (((1,), (1,)), ((), ())),
        preferred_element_type=jnp.float32,
    )
    token_gradient = (
        frozen_input_gradient + adapter_input_gradient.reshape(token_rows, width_portion)
    ).astype(jnp.bfloat16)
    return (projected, token_gradient, grad_down, grad_up)


def solution(mesh):
    return jax.shard_map(
        per_device,
        mesh=mesh,
        in_specs=(
            P("tok", "tp"),
            P("tp", None),
            P("tok", "tp", None),
            P("tok", None, "tp"),
            P("tok"),
            P(),
            P(),
            P("tok", "tp"),
        ),
        out_specs=(P("tok", "tp"), P("tok", "tp"), P("tok", "tp", None), P("tok", None, "tp")),
        check_vma=False,
    )
```

```python
import jax
import jax.numpy as jnp
from jax import lax
from jax.sharding import PartitionSpec as P

ALPHA = 32
BLOCK_TOKENS = 16


def per_device(
    tokens,
    frozen_weight,
    adapter_down_matrices,
    adapter_up_matrices,
    adapter_per_block,
    slot_per_adapter,
    rank_per_adapter,
    output_gradient,
):
    tok_count = lax.axis_size("tok")
    token_rows = tokens.shape[0]
    width_portion = tokens.shape[1]
    column_portion = output_gradient.shape[1]
    block_count = adapter_per_block.shape[0]
    number_adapters = adapter_down_matrices.shape[0]
    rank_ceiling = adapter_down_matrices.shape[2]
    capacity = max(2, 2 * block_count // tok_count)
    storage_position_count = tok_count * capacity
    adapter_total = slot_per_adapter.shape[0]
    weight_cols = frozen_weight
    base_out = lax.psum_scatter(
        lax.dot_general(
            weight_cols, tokens, (((0,), (1,)), ((), ())), preferred_element_type=jnp.float32
        ),
        "tp",
        scatter_dimension=0,
        tiled=True,
    ).T
    adapter_ids = jnp.arange(adapter_total, dtype=jnp.int32)
    matches = adapter_per_block[:, None] == adapter_ids[None, :]
    block_slot = jnp.sum(jnp.where(matches, slot_per_adapter[None, :], 0), axis=1)
    owner_ids = block_slot // number_adapters
    local_index = block_slot % number_adapters
    block_ids = jnp.arange(block_count, dtype=jnp.int32)
    earlier = (owner_ids[:, None] == owner_ids[None, :]) & (block_ids[None, :] < block_ids[:, None])
    position = jnp.sum(earlier.astype(jnp.int32), axis=1)
    destination = owner_ids * capacity + position
    placement = jnp.arange(storage_position_count, dtype=jnp.int32)[:, None] == destination[None, :]
    place_matrix = placement.astype(jnp.bfloat16)
    send_rows = jnp.dot(
        place_matrix,
        tokens.reshape(block_count, BLOCK_TOKENS * width_portion),
        preferred_element_type=jnp.float32,
    ).astype(jnp.bfloat16)
    send_grads = jnp.dot(
        place_matrix,
        output_gradient.reshape(block_count, BLOCK_TOKENS * column_portion),
        preferred_element_type=jnp.float32,
    ).astype(jnp.bfloat16)
    slot_adapter = jnp.sum(jnp.where(placement, local_index[None, :] + 1, 0), axis=1) - 1
    tag = jnp.zeros((storage_position_count, BLOCK_TOKENS, 128), jnp.bfloat16)
    tag = tag.at[:, 0, 0].set((slot_adapter + 1).astype(jnp.bfloat16))
    tagged_grads = jnp.concatenate(
        [send_grads.reshape(storage_position_count, BLOCK_TOKENS, column_portion), tag], axis=2
    )
    arrived_tagged = lax.all_to_all(tagged_grads, "tok", split_axis=0, concat_axis=0, tiled=True)
    send_rows, arrived_tagged = lax.optimization_barrier((send_rows, arrived_tagged))
    arrived_rows = lax.all_to_all(
        send_rows.reshape(storage_position_count, BLOCK_TOKENS, width_portion),
        "tok",
        split_axis=0,
        concat_axis=0,
        tiled=True,
    )
    arrived_grads = arrived_tagged[:, :, :column_portion]
    arrived_adapter = arrived_tagged[:, 0, column_portion].astype(jnp.int32) - 1
    row_total = storage_position_count * BLOCK_TOKENS
    input_row_block = arrived_rows.reshape(row_total, width_portion)
    gradient_row_block = arrived_grads.reshape(row_total, column_portion)
    chosen = arrived_adapter[:, None] == jnp.arange(number_adapters, dtype=jnp.int32)[None, :]
    chosen_rows = jnp.broadcast_to(
        chosen[:, None, :], (storage_position_count, BLOCK_TOKENS, number_adapters)
    ).reshape(row_total, number_adapters)
    chosen_float = chosen_rows.astype(jnp.float32)
    chosen_half = chosen_rows.astype(jnp.bfloat16)
    stored_ids = lax.axis_index("tok") * number_adapters + jnp.arange(
        number_adapters, dtype=jnp.int32
    )
    stored_match = slot_per_adapter[None, :] == stored_ids[:, None]
    stored_rank = jnp.sum(jnp.where(stored_match, rank_per_adapter[None, :], 0), axis=1)
    stored_scale = jnp.where(
        stored_rank > 0, jnp.float32(ALPHA) / jnp.maximum(stored_rank, 1).astype(jnp.float32), 0.0
    )
    row_rank = jnp.sum(jnp.where(chosen_rows, stored_rank[None, :], 0), axis=1)
    scale_per_row = jnp.sum(chosen_float * stored_scale[None, :], axis=1)
    keep_cols = jnp.arange(rank_ceiling, dtype=jnp.int32)[None, :] < row_rank[:, None]
    reduced_every_row = jnp.einsum(
        "ue,meb->umb", input_row_block, adapter_down_matrices, preferred_element_type=jnp.float32
    )
    low_part = jnp.sum(reduced_every_row * chosen_float[:, :, None], axis=1)
    gathered_every_row = jnp.einsum(
        "hs,gbs->hgb", gradient_row_block, adapter_up_matrices, preferred_element_type=jnp.float32
    )
    pull_part = jnp.sum(gathered_every_row * chosen_float[:, :, None], axis=1)
    low_sum, pull_sum = lax.psum((low_part, pull_part), "tp")
    reduced_rows = jnp.where(keep_cols, low_sum, 0.0).astype(jnp.bfloat16)
    reduced_gradient = (scale_per_row[:, None] * jnp.where(keep_cols, pull_sum, 0.0)).astype(
        jnp.bfloat16
    )
    reduced_picked = chosen_half[:, :, None] * reduced_rows[:, None, :]
    gradient_picked = chosen_half[:, :, None] * reduced_gradient[:, None, :]
    adapter_increment = scale_per_row[:, None] * jnp.einsum(
        "hnq,nqs->hs", reduced_picked, adapter_up_matrices, preferred_element_type=jnp.float32
    )
    grad_down = jnp.einsum(
        "rd,rak->adk", input_row_block, gradient_picked, preferred_element_type=jnp.float32
    )
    grad_up = stored_scale[:, None, None] * jnp.einsum(
        "rak,rc->akc", reduced_picked, gradient_row_block, preferred_element_type=jnp.float32
    )
    adapter_output_rows = jnp.einsum(
        "ymf,mcf->yc", gradient_picked, adapter_down_matrices, preferred_element_type=jnp.float32
    )
    delta_back, row_input_gradient = (
        lax.all_to_all(
            adapter_increment.reshape(storage_position_count, BLOCK_TOKENS, column_portion),
            "tok",
            split_axis=0,
            concat_axis=0,
            tiled=True,
        ),
        lax.all_to_all(
            adapter_output_rows.reshape(storage_position_count, BLOCK_TOKENS, width_portion),
            "tok",
            split_axis=0,
            concat_axis=0,
            tiled=True,
        ),
    )
    adapter_input_gradient = jnp.take(row_input_gradient, destination, axis=0)
    mine_delta = jnp.take(delta_back, destination, axis=0)
    projected = (base_out + mine_delta.reshape(token_rows, column_portion)).astype(jnp.bfloat16)
    weight_cols = frozen_weight
    frozen_input_gradient = lax.dot_general(
        lax.all_gather(output_gradient, "tp", axis=1, tiled=True),
        weight_cols,
        (((1,), (1,)), ((), ())),
        preferred_element_type=jnp.float32,
    )
    token_gradient = (
        frozen_input_gradient + adapter_input_gradient.reshape(token_rows, width_portion)
    ).astype(jnp.bfloat16)
    return (projected, token_gradient, grad_down, grad_up)


def solution(mesh):
    return jax.shard_map(
        per_device,
        mesh=mesh,
        in_specs=(
            P("tok", "tp"),
            P("tp", None),
            P("tok", "tp", None),
            P("tok", None, "tp"),
            P("tok"),
            P(),
            P(),
            P("tok", "tp"),
        ),
        out_specs=(P("tok", "tp"), P("tok", "tp"), P("tok", "tp", None), P("tok", None, "tp")),
        check_vma=False,
    )
```

```python
import jax
import jax.numpy as jnp
from jax import lax
from jax.sharding import PartitionSpec as P

ALPHA = 32
BLOCK_TOKENS = 16


def per_device(
    tokens,
    frozen_weight,
    adapter_down_matrices,
    adapter_up_matrices,
    adapter_per_block,
    slot_per_adapter,
    rank_per_adapter,
    output_gradient,
):
    tok_count = lax.axis_size("tok")
    token_rows = tokens.shape[0]
    width_portion = tokens.shape[1]
    column_portion = output_gradient.shape[1]
    block_count = adapter_per_block.shape[0]
    number_adapters = adapter_down_matrices.shape[0]
    rank_ceiling = adapter_down_matrices.shape[2]
    capacity = max(2, 2 * block_count // tok_count)
    storage_position_count = tok_count * capacity
    adapter_total = slot_per_adapter.shape[0]
    weight_cols = frozen_weight
    base_out = lax.psum_scatter(
        lax.dot_general(
            weight_cols, tokens, (((0,), (1,)), ((), ())), preferred_element_type=jnp.float32
        ),
        "tp",
        scatter_dimension=0,
        tiled=True,
    ).T
    adapter_ids = jnp.arange(adapter_total, dtype=jnp.int32)
    matches = adapter_per_block[:, None] == adapter_ids[None, :]
    block_slot = jnp.sum(jnp.where(matches, slot_per_adapter[None, :], 0), axis=1)
    owner_ids = block_slot // number_adapters
    local_index = block_slot % number_adapters
    block_ids = jnp.arange(block_count, dtype=jnp.int32)
    earlier = (owner_ids[:, None] == owner_ids[None, :]) & (block_ids[None, :] < block_ids[:, None])
    position = jnp.sum(earlier.astype(jnp.int32), axis=1)
    destination = owner_ids * capacity + position
    placement = jnp.arange(storage_position_count, dtype=jnp.int32)[:, None] == destination[None, :]
    place_matrix = placement.astype(jnp.bfloat16)
    send_rows = jnp.dot(
        place_matrix,
        tokens.reshape(block_count, BLOCK_TOKENS * width_portion),
        preferred_element_type=jnp.float32,
    ).astype(jnp.bfloat16)
    send_grads = jnp.dot(
        place_matrix,
        output_gradient.reshape(block_count, BLOCK_TOKENS * column_portion),
        preferred_element_type=jnp.float32,
    ).astype(jnp.bfloat16)
    slot_adapter = jnp.sum(jnp.where(placement, local_index[None, :] + 1, 0), axis=1) - 1
    tag = jnp.zeros((storage_position_count, 128), jnp.bfloat16)
    tag = tag.at[:, 0].set((slot_adapter + 1).astype(jnp.bfloat16))
    tagged_grads = jnp.concatenate([send_grads, tag], axis=1)
    arrived_tagged = lax.all_to_all(tagged_grads, "tok", split_axis=0, concat_axis=0, tiled=True)
    send_rows, arrived_tagged = lax.optimization_barrier((send_rows, arrived_tagged))
    arrived_rows = lax.all_to_all(
        send_rows.reshape(storage_position_count, BLOCK_TOKENS, width_portion),
        "tok",
        split_axis=0,
        concat_axis=0,
        tiled=True,
    )
    arrived_grads = arrived_tagged[:, : BLOCK_TOKENS * column_portion]
    arrived_adapter = arrived_tagged[:, BLOCK_TOKENS * column_portion].astype(jnp.int32) - 1
    row_total = storage_position_count * BLOCK_TOKENS
    input_row_block = arrived_rows.reshape(row_total, width_portion)
    gradient_row_block = arrived_grads.reshape(row_total, column_portion)
    chosen = arrived_adapter[:, None] == jnp.arange(number_adapters, dtype=jnp.int32)[None, :]
    chosen_rows = jnp.broadcast_to(
        chosen[:, None, :], (storage_position_count, BLOCK_TOKENS, number_adapters)
    ).reshape(row_total, number_adapters)
    chosen_float = chosen_rows.astype(jnp.float32)
    chosen_half = chosen_rows.astype(jnp.bfloat16)
    stored_ids = lax.axis_index("tok") * number_adapters + jnp.arange(
        number_adapters, dtype=jnp.int32
    )
    stored_match = slot_per_adapter[None, :] == stored_ids[:, None]
    stored_rank = jnp.sum(jnp.where(stored_match, rank_per_adapter[None, :], 0), axis=1)
    stored_scale = jnp.where(
        stored_rank > 0, jnp.float32(ALPHA) / jnp.maximum(stored_rank, 1).astype(jnp.float32), 0.0
    )
    row_rank = jnp.sum(jnp.where(chosen_rows, stored_rank[None, :], 0), axis=1)
    scale_per_row = jnp.sum(chosen_float * stored_scale[None, :], axis=1)
    keep_cols = jnp.arange(rank_ceiling, dtype=jnp.int32)[None, :] < row_rank[:, None]
    reduced_every_row = jnp.einsum(
        "ue,meb->umb", input_row_block, adapter_down_matrices, preferred_element_type=jnp.float32
    )
    low_part = jnp.sum(reduced_every_row * chosen_float[:, :, None], axis=1)
    gathered_every_row = jnp.einsum(
        "hs,gbs->hgb", gradient_row_block, adapter_up_matrices, preferred_element_type=jnp.float32
    )
    pull_part = jnp.sum(gathered_every_row * chosen_float[:, :, None], axis=1)
    low_sum, pull_sum = lax.psum((low_part, pull_part), "tp")
    reduced_rows = jnp.where(keep_cols, low_sum, 0.0).astype(jnp.bfloat16)
    reduced_gradient = (scale_per_row[:, None] * jnp.where(keep_cols, pull_sum, 0.0)).astype(
        jnp.bfloat16
    )
    reduced_picked = chosen_half[:, :, None] * reduced_rows[:, None, :]
    gradient_picked = chosen_half[:, :, None] * reduced_gradient[:, None, :]
    adapter_increment = scale_per_row[:, None] * jnp.einsum(
        "hnq,nqs->hs", reduced_picked, adapter_up_matrices, preferred_element_type=jnp.float32
    )
    grad_down = jnp.einsum(
        "rd,rak->adk", input_row_block, gradient_picked, preferred_element_type=jnp.float32
    )
    grad_up = stored_scale[:, None, None] * jnp.einsum(
        "rak,rc->akc", reduced_picked, gradient_row_block, preferred_element_type=jnp.float32
    )
    adapter_output_rows = jnp.einsum(
        "ymf,mcf->yc", gradient_picked, adapter_down_matrices, preferred_element_type=jnp.float32
    )
    delta_back, row_input_gradient = (
        lax.all_to_all(
            adapter_increment.reshape(storage_position_count, BLOCK_TOKENS, column_portion),
            "tok",
            split_axis=0,
            concat_axis=0,
            tiled=True,
        ),
        lax.all_to_all(
            adapter_output_rows.reshape(storage_position_count, BLOCK_TOKENS, width_portion),
            "tok",
            split_axis=0,
            concat_axis=0,
            tiled=True,
        ),
    )
    adapter_input_gradient = jnp.take(row_input_gradient, destination, axis=0)
    mine_delta = jnp.take(delta_back, destination, axis=0)
    projected = (base_out + mine_delta.reshape(token_rows, column_portion)).astype(jnp.bfloat16)
    weight_cols = frozen_weight
    frozen_input_gradient = lax.dot_general(
        lax.all_gather(output_gradient, "tp", axis=1, tiled=True),
        weight_cols,
        (((1,), (1,)), ((), ())),
        preferred_element_type=jnp.float32,
    )
    token_gradient = (
        frozen_input_gradient + adapter_input_gradient.reshape(token_rows, width_portion)
    ).astype(jnp.bfloat16)
    return (projected, token_gradient, grad_down, grad_up)


def solution(mesh):
    return jax.shard_map(
        per_device,
        mesh=mesh,
        in_specs=(
            P("tok", "tp"),
            P("tp", None),
            P("tok", "tp", None),
            P("tok", None, "tp"),
            P("tok"),
            P(),
            P(),
            P("tok", "tp"),
        ),
        out_specs=(P("tok", "tp"), P("tok", "tp"), P("tok", "tp", None), P("tok", None, "tp")),
        check_vma=False,
    )
```
